256 devices in a mesh: tm: 32 (over z, x_hi, core), chan: 8 (over y, x_lo).
Axes of the slice: x: 4 (x_hi: 2, x_lo: 2; x = x_hi * 2 + x_lo), y: 4, z: 8, core: 2. Of those that a mesh axis runs over, the one named last changes fastest.
Arguments:
- states: bfloat16 [2, 8192, 2048], P(None, 'tm'), may hold values from -6 to 6
- upstream: bfloat16 [2, 8192, 2048], P(None, 'tm'), may hold values from -6 to 6
- w_in: bfloat16 [2, 2, 2048, 2048], P(None, None, None, 'chan'), may hold values from -0.09375 to 0.09375
- w_out: bfloat16 [2048, 2048], P('chan'), may hold values from -0.125 to 0.125
- lengths: int32 [2], replicated, may hold values from 2048 to 8192, as said below
Outputs:
- grad_states: bfloat16 [2, 8192, 2048], P(None, 'tm', 'chan')
- grad_in: float32 [2, 2, 2048, 2048], P(None, None, 'tm', 'chan')
- grad_out: float32 [2048, 2048], P('chan', 'tm')
The draws below stay inside these ranges and needn't reach their ends.
Inputs may be any that keep to these rules, and one draw needn't show every extreme that they name: `lengths`: one trajectory has all 8192 steps valid, the other at least a quarter of them.
All inputs are finite; a program needn't handle non-finite values.
Results may differ from the reference program's by a relative error of at most 0.0029.
Values may be sent and summed in bfloat16 or wider, within the bound.
No kernel may reach another device: no remote copies, remote signals or barrier semaphores. Data moves between devices by JAX's collectives and lax.ppermute only.
A program may use at most 128 MiB of HBM per device.

```python
import jax
import jax.numpy as jnp
from jax import lax

RESIDUAL_WIDTH = 2048
BLOCK_CHANNELS = 2048
DILATION_STEPS = 1024
TRAJ = 2
TIME_STEPS = 8192


def draw_lengths(key, part):
    first_key, second_key = jax.random.split(jax.random.fold_in(key, 11))
    longest = jax.random.randint(first_key, (), 0, TRAJ)
    others = jax.random.randint(second_key, (TRAJ,), TIME_STEPS // 4, TIME_STEPS + 1)
    slots = jnp.arange(TRAJ, dtype=jnp.int32)
    return jnp.where(slots == longest, TIME_STEPS, others).astype(jnp.int32)


def strengthened(values, stream_key, source, target, blocks, factor):
    owner, partner = [(jnp.arange(values.shape[position]) // (values.shape[position] // blocks)).reshape([-1 if axis == position else 1 for axis in range(values.ndim)]) for position in (source, target)]
    chosen = jax.random.permutation(stream_key, blocks)[partner]
    strong = (owner == chosen) | (owner == (partner + blocks // 2) % blocks)
    return jnp.where(strong, factor * values, values)


def shard_levels(stream_key, extent, shards, smallest, largest):
    def one(axis_at, shards_of):
        heights = jax.random.uniform(jax.random.fold_in(jax.random.fold_in(stream_key, 6), axis_at), (shards_of,), jnp.float32, smallest / len(shards), largest / len(shards))
        return jnp.repeat(jnp.exp(heights), extent[axis_at] // shards_of).reshape((-1,) + (1,) * (len(extent) - axis_at - 1))

    level = one(*shards[0])
    for cut in shards[1:]:
        level = level * one(*cut)
    return level


def noise(rng, shape, deviation, reach, cuts=(), kind=jnp.bfloat16):
    values = deviation * jax.random.normal(rng, shape, jnp.float32)
    if cuts:
        values = values * shard_levels(rng, shape, cuts, -0.22, 0.18)
    return jnp.clip(values, -reach, reach).astype(kind)


def noise_with(rng, shape, width, most, pieces, heavy, held_as=jnp.bfloat16):
    values = width * jax.random.normal(rng, shape, jnp.float32)
    if pieces:
        values = values * shard_levels(rng, shape, pieces, -0.22, 0.18)
    return jnp.clip(strengthened(values, jax.random.fold_in(rng, 3), *heavy), -most, most).astype(held_as)


def setup_inputs(seed: int = 0) -> dict:
    arg_keys = jax.random.split(jax.random.key(seed), 6)
    states = noise_with(arg_keys[0], (TRAJ, TIME_STEPS, RESIDUAL_WIDTH), 1.0, 6.0, ((1, 32),), (1, 2, 32, 2.75))
    upstream = noise(arg_keys[1], (TRAJ, TIME_STEPS, RESIDUAL_WIDTH), 1.0, 6.0, ((1, 32),))
    w_in = noise(arg_keys[2], (2, 2, RESIDUAL_WIDTH, BLOCK_CHANNELS), (2 * RESIDUAL_WIDTH) ** -0.5, 0.09375, ((3, 8),))
    w_out = noise(arg_keys[3], (BLOCK_CHANNELS, RESIDUAL_WIDTH), BLOCK_CHANNELS ** -0.5, 0.125, ((0, 8),))
    lengths = draw_lengths(jax.random.fold_in(arg_keys[5], 71), 0)
    return dict(states=states, upstream=upstream, w_in=w_in, w_out=w_out, lengths=lengths)


def reference(states, upstream, w_in, w_out, lengths):
    blank_rows = jnp.zeros((DILATION_STEPS, RESIDUAL_WIDTH), jnp.bfloat16)
    blank_gradients = jnp.zeros((DILATION_STEPS, BLOCK_CHANNELS), jnp.bfloat16)
    positions = jnp.arange(TIME_STEPS, dtype=jnp.int32)
    grad_in = jnp.zeros((2, 2, RESIDUAL_WIDTH, BLOCK_CHANNELS), jnp.float32)
    grad_out = jnp.zeros((BLOCK_CHANNELS, RESIDUAL_WIDTH), jnp.float32)
    outputs = []
    for index in range(TRAJ):
        present_step = states[index]
        previous_step = jnp.concatenate([blank_rows, present_step[:TIME_STEPS - DILATION_STEPS]], axis=0)
        filt = jnp.dot(present_step, w_in[0, 0], preferred_element_type=jnp.float32) + jnp.dot(previous_step, w_in[1, 0], preferred_element_type=jnp.float32)
        gate = jnp.dot(present_step, w_in[0, 1], preferred_element_type=jnp.float32) + jnp.dot(previous_step, w_in[1, 1], preferred_element_type=jnp.float32)
        tangent = jnp.tanh(filt)
        sigma = jax.nn.sigmoid(gate)
        mixed = (tangent * sigma).astype(jnp.bfloat16)
        valid = positions < lengths[index]
        grad_rows = jnp.where(valid[:, None], upstream[index], jnp.zeros_like(upstream[index]))
        dmix = jnp.dot(grad_rows, w_out.T, preferred_element_type=jnp.float32)
        filter_gradient = (dmix * (1.0 - tangent * tangent) * sigma).astype(jnp.bfloat16)
        gate_gradient = (dmix * tangent * sigma * (1.0 - sigma)).astype(jnp.bfloat16)
        following_filter = jnp.concatenate([filter_gradient[DILATION_STEPS:], blank_gradients], axis=0)
        following_gate = jnp.concatenate([gate_gradient[DILATION_STEPS:], blank_gradients], axis=0)
        total = grad_rows.astype(jnp.float32)
        total = total + jnp.dot(filter_gradient, w_in[0, 0].T, preferred_element_type=jnp.float32)
        total = total + jnp.dot(gate_gradient, w_in[0, 1].T, preferred_element_type=jnp.float32)
        total = total + jnp.dot(following_filter, w_in[1, 0].T, preferred_element_type=jnp.float32)
        total = total + jnp.dot(following_gate, w_in[1, 1].T, preferred_element_type=jnp.float32)
        outputs.append(total.astype(jnp.bfloat16))
        terms = jnp.stack([jnp.stack([jnp.dot(present_step.T, filter_gradient, preferred_element_type=jnp.float32), jnp.dot(present_step.T, gate_gradient, preferred_element_type=jnp.float32)]), jnp.stack([jnp.dot(previous_step.T, filter_gradient, preferred_element_type=jnp.float32), jnp.dot(previous_step.T, gate_gradient, preferred_element_type=jnp.float32)])])
        grad_in = grad_in + terms
        grad_out = grad_out + jnp.dot(mixed.T, grad_rows, preferred_element_type=jnp.float32)
    scale = lax.rsqrt(jnp.sum(lengths.astype(jnp.float32)))
    return (jnp.stack(outputs), grad_in * scale, grad_out * scale)
```

```python
import jax
import jax.numpy as jnp
from jax import lax
from jax.sharding import PartitionSpec as P

DILATION_STEPS = 1024


def shifted(x, axis, by):
    peers = lax.axis_size(axis)
    pairs = [(i, i + by) for i in range(peers) if 0 <= i + by < peers]
    return lax.ppermute(x, axis, pairs)


def contract_rows(left, right):
    return lax.dot_general(
        left, right, (((0,), (0,)), ((), ())), preferred_element_type=jnp.float32
    )


def contract_cols(left, right):
    return lax.dot_general(
        left, right, (((1,), (1,)), ((), ())), preferred_element_type=jnp.float32
    )


def local(states, upstream, w_in, w_out, lengths):
    traj, window_extent, width = states.shape
    blocks = w_in.shape[3]
    rows_n = traj * window_extent
    receptive_extent = DILATION_STEPS // window_extent
    rows = states.reshape(rows_n, width)
    w_now = jnp.concatenate([w_in[0, 0], w_in[0, 1]], axis=1)
    w_dil = jnp.concatenate([w_in[1, 0], w_in[1, 1]], axis=1)
    dilated = jnp.dot(rows, w_dil, preferred_element_type=jnp.float32)
    dilated_prior = shifted(
        dilated.reshape(traj, window_extent, 2 * blocks), "tm", receptive_extent
    ).reshape(rows_n, 2 * blocks)
    pre = jnp.dot(rows, w_now, preferred_element_type=jnp.float32) + dilated_prior
    filt = pre[:, :blocks]
    gate = pre[:, blocks:]
    first = lax.axis_index("tm") * window_extent
    positions = first + jnp.arange(window_extent, dtype=jnp.int32)
    valid = positions[None, :] < lengths[:, None]
    grad_rows = jnp.where(valid[:, :, None], upstream, jnp.zeros_like(upstream))
    grad_flat = grad_rows.reshape(rows_n, width)
    tangent = jnp.tanh(filt)
    sigma = jax.nn.sigmoid(gate)
    mixed = (tangent * sigma).astype(jnp.bfloat16)
    dmix = contract_cols(grad_flat, w_out)
    filter_gradient = (dmix * (1.0 - tangent * tangent) * sigma).astype(jnp.bfloat16)
    gate_gradient = (dmix * tangent * sigma * (1.0 - sigma)).astype(jnp.bfloat16)
    branch_grads = jnp.concatenate([filter_gradient, gate_gradient], axis=1)
    later = shifted(
        branch_grads.reshape(traj, window_extent, 2 * blocks), "tm", -receptive_extent
    ).reshape(rows_n, 2 * blocks)
    partial_value = contract_cols(w_now, branch_grads) + contract_cols(w_dil, later)
    summed = lax.psum_scatter(partial_value, "chan", scatter_dimension=0, tiled=True)
    share = width // lax.axis_size("chan")
    own_rows = lax.dynamic_slice_in_dim(grad_rows, lax.axis_index("chan") * share, share, 2)
    summed = summed.reshape(share, traj, window_extent).transpose(1, 2, 0)
    grad_states = (own_rows.astype(jnp.float32) + summed).astype(jnp.bfloat16)
    weight_terms = jnp.concatenate(
        [
            contract_rows(rows, branch_grads),
            contract_rows(rows, later),
            contract_rows(grad_flat, mixed),
        ],
        axis=1,
    )
    reduced = lax.psum_scatter(weight_terms, "tm", scatter_dimension=0, tiled=True)
    scale = lax.rsqrt(jnp.sum(lengths.astype(jnp.float32)))
    part = reduced.shape[0]
    in_summed = reduced[:, : 4 * blocks].reshape(part, 2, 2, blocks).transpose(1, 2, 0, 3)
    out_summed = reduced[:, 4 * blocks :].T
    return (grad_states, in_summed * scale, out_summed * scale)


def solution(mesh):
    placed = (
        P(None, "tm", None),
        P(None, "tm", None),
        P(None, None, None, "chan"),
        P("chan", None),
        P(),
    )
    return jax.shard_map(
        local,
        mesh=mesh,
        in_specs=placed,
        out_specs=(P(None, "tm", "chan"), P(None, None, "tm", "chan"), P("chan", "tm")),
        check_vma=False,
    )
```

```python
import jax
import jax.numpy as jnp
from jax import lax
from jax.sharding import PartitionSpec as P

DILATION_STEPS = 1024


TIME = ("outer", "core")


def shifted(x, axis, by):
    peers = lax.axis_size(axis[0]) * lax.axis_size(axis[1])
    pairs = [(i, i + by) for i in range(peers) if 0 <= i + by < peers]
    return lax.ppermute(x, axis, pairs)


def contract_rows(left, right):
    return lax.dot_general(
        left, right, (((0,), (0,)), ((), ())), preferred_element_type=jnp.float32
    )


def contract_cols(left, right):
    return lax.dot_general(
        left, right, (((1,), (1,)), ((), ())), preferred_element_type=jnp.float32
    )


def local(states, upstream, w_in, w_out, lengths):
    traj, window_extent, width = states.shape
    blocks = w_in.shape[3]
    rows_n = traj * window_extent
    receptive_extent = DILATION_STEPS // window_extent
    rows = states.reshape(rows_n, width)
    w_now = jnp.concatenate([w_in[0, 0], w_in[0, 1]], axis=1)
    w_dil = jnp.concatenate([w_in[1, 0], w_in[1, 1]], axis=1)
    dilated = jnp.dot(rows, w_dil, preferred_element_type=jnp.float32)
    dilated_prior = shifted(
        dilated.reshape(traj, window_extent, 2 * blocks), TIME, receptive_extent
    ).reshape(rows_n, 2 * blocks)
    pre = jnp.dot(rows, w_now, preferred_element_type=jnp.float32) + dilated_prior
    filt = pre[:, :blocks]
    gate = pre[:, blocks:]
    first = lax.axis_index(TIME) * window_extent
    positions = first + jnp.arange(window_extent, dtype=jnp.int32)
    valid = positions[None, :] < lengths[:, None]
    grad_rows = jnp.where(valid[:, :, None], upstream, jnp.zeros_like(upstream))
    grad_flat = grad_rows.reshape(rows_n, width)
    tangent = jnp.tanh(filt)
    sigma = jax.nn.sigmoid(gate)
    mixed = (tangent * sigma).astype(jnp.bfloat16)
    dmix = contract_cols(grad_flat, w_out)
    filter_gradient = (dmix * (1.0 - tangent * tangent) * sigma).astype(jnp.bfloat16)
    gate_gradient = (dmix * tangent * sigma * (1.0 - sigma)).astype(jnp.bfloat16)
    branch_grads = jnp.concatenate([filter_gradient, gate_gradient], axis=1)
    later = shifted(
        branch_grads.reshape(traj, window_extent, 2 * blocks), TIME, -receptive_extent
    ).reshape(rows_n, 2 * blocks)
    partial_value = contract_cols(w_now, branch_grads) + contract_cols(w_dil, later)
    summed = lax.psum_scatter(
        partial_value.astype(jnp.bfloat16), "chan", scatter_dimension=0, tiled=True
    ).astype(jnp.float32)
    share = width // lax.axis_size("chan")
    own_rows = lax.dynamic_slice_in_dim(grad_rows, lax.axis_index("chan") * share, share, 2)
    summed = summed.reshape(share, traj, window_extent).transpose(1, 2, 0)
    grad_states = (own_rows.astype(jnp.float32) + summed).astype(jnp.bfloat16)
    weight_terms = jnp.concatenate(
        [
            contract_rows(rows, branch_grads),
            contract_rows(rows, later),
            contract_rows(grad_flat, mixed),
        ],
        axis=1,
    )
    pair = lax.axis_index("core")
    halves = weight_terms.reshape(lax.axis_size("outer"), 2, -1, weight_terms.shape[1])
    keep = lax.dynamic_index_in_dim(halves, pair, axis=1, keepdims=False)
    give = lax.dynamic_index_in_dim(halves, 1 - pair, axis=1, keepdims=False)
    paired = keep + lax.ppermute(give, "core", [(0, 1), (1, 0)])
    reduced = lax.psum_scatter(
        paired.reshape(-1, weight_terms.shape[1]), "outer", scatter_dimension=0, tiled=True
    )
    scale = lax.rsqrt(jnp.sum(lengths.astype(jnp.float32)))
    part = reduced.shape[0]
    in_summed = reduced[:, : 4 * blocks].reshape(part, 2, 2, blocks).transpose(1, 2, 0, 3)
    out_summed = reduced[:, 4 * blocks :].T
    return (grad_states, in_summed * scale, out_summed * scale)


def solution(mesh):
    tm, chan = mesh.shape["tm"], mesh.shape["chan"]
    mesh = jax.sharding.Mesh(
        mesh.devices.reshape(tm // 2, 2, chan), ("outer", "core", "chan")
    )
    placed = (
        P(None, TIME, None),
        P(None, TIME, None),
        P(None, None, None, "chan"),
        P("chan", None),
        P(),
    )
    return jax.shard_map(
        local,
        mesh=mesh,
        in_specs=placed,
        out_specs=(P(None, TIME, "chan"), P(None, None, TIME, "chan"), P("chan", TIME)),
        check_vma=False,
    )
```

```python
import jax
import jax.numpy as jnp
from jax import lax
from jax.sharding import PartitionSpec as P

DILATION_STEPS = 1024


def shifted(x, axis, by):
    peers = lax.axis_size(axis)
    pairs = [(i, i + by) for i in range(peers) if 0 <= i + by < peers]
    return lax.ppermute(x, axis, pairs)


def contract_rows(left, right):
    return lax.dot_general(
        left, right, (((0,), (0,)), ((), ())), preferred_element_type=jnp.float32
    )


def contract_cols(left, right):
    return lax.dot_general(
        left, right, (((1,), (1,)), ((), ())), preferred_element_type=jnp.float32
    )


def ring_reduce_scatter(x):
    peers = lax.axis_size("ring")
    at = lax.axis_index("ring")
    chunks = x.reshape(peers, x.shape[0] // peers, x.shape[1])
    half = x.shape[1] // 2
    sums = []
    for step, cols in ((1, slice(0, half)), (-1, slice(half, None))):
        own = chunks[:, :, cols]
        pairs = [(i, (i + step) % peers) for i in range(peers)]
        acc = lax.dynamic_index_in_dim(own, (at - step) % peers, 0, keepdims=False)
        for s in range(peers - 1):
            got = lax.ppermute(acc, "ring", pairs)
            acc = got + lax.dynamic_index_in_dim(
                own, (at - step * (s + 2)) % peers, 0, keepdims=False
            )
        sums.append(acc)
    full = jnp.concatenate(sums, axis=1)
    pairs_n = lax.axis_size("pair")
    me = lax.axis_index("pair")
    parts = full.reshape(pairs_n, full.shape[0] // pairs_n, full.shape[1])
    keep = lax.dynamic_index_in_dim(parts, me, 0, keepdims=False)
    give = lax.dynamic_index_in_dim(parts, 1 - me, 0, keepdims=False)
    return keep + lax.ppermute(give, "pair", [(0, 1), (1, 0)])


def local(states, upstream, w_in, w_out, lengths):
    traj, window_extent, width = states.shape
    blocks = w_in.shape[3]
    rows_n = traj * window_extent
    receptive_extent = DILATION_STEPS // window_extent
    rows = states.reshape(rows_n, width)
    w_now = jnp.concatenate([w_in[0, 0], w_in[0, 1]], axis=1)
    w_dil = jnp.concatenate([w_in[1, 0], w_in[1, 1]], axis=1)
    dilated = jnp.dot(rows, w_dil, preferred_element_type=jnp.float32)
    dilated_prior = shifted(
        dilated.reshape(traj, window_extent, 2 * blocks), "tm", receptive_extent
    ).reshape(rows_n, 2 * blocks)
    pre = jnp.dot(rows, w_now, preferred_element_type=jnp.float32) + dilated_prior
    filt = pre[:, :blocks]
    gate = pre[:, blocks:]
    first = lax.axis_index("tm") * window_extent
    positions = first + jnp.arange(window_extent, dtype=jnp.int32)
    valid = positions[None, :] < lengths[:, None]
    grad_rows = jnp.where(valid[:, :, None], upstream, jnp.zeros_like(upstream))
    grad_flat = grad_rows.reshape(rows_n, width)
    tangent = jnp.tanh(filt)
    sigma = jax.nn.sigmoid(gate)
    mixed = (tangent * sigma).astype(jnp.bfloat16)
    dmix = contract_cols(grad_flat, w_out)
    filter_gradient = (dmix * (1.0 - tangent * tangent) * sigma).astype(jnp.bfloat16)
    gate_gradient = (dmix * tangent * sigma * (1.0 - sigma)).astype(jnp.bfloat16)
    branch_grads = jnp.concatenate([filter_gradient, gate_gradient], axis=1)
    later = shifted(
        branch_grads.reshape(traj, window_extent, 2 * blocks), "tm", -receptive_extent
    ).reshape(rows_n, 2 * blocks)
    partial_value = contract_cols(w_now, branch_grads) + contract_cols(w_dil, later)
    summed = ring_reduce_scatter(partial_value)
    share = width // (lax.axis_size("ring") * lax.axis_size("pair"))
    chan_index = lax.axis_index("ring") * lax.axis_size("pair") + lax.axis_index("pair")
    own_rows = lax.dynamic_slice_in_dim(grad_rows, chan_index * share, share, 2)
    summed = summed.reshape(share, traj, window_extent).transpose(1, 2, 0)
    grad_states = (own_rows.astype(jnp.float32) + summed).astype(jnp.bfloat16)
    weight_terms = jnp.concatenate(
        [
            contract_rows(rows, branch_grads),
            contract_rows(rows, later),
            contract_rows(grad_flat, mixed),
        ],
        axis=1,
    )
    reduced = lax.psum_scatter(weight_terms, "tm", scatter_dimension=0, tiled=True)
    scale = lax.rsqrt(jnp.sum(lengths.astype(jnp.float32)))
    part = reduced.shape[0]
    in_summed = reduced[:, : 4 * blocks].reshape(part, 2, 2, blocks).transpose(1, 2, 0, 3)
    out_summed = reduced[:, 4 * blocks :].T
    return (grad_states, in_summed * scale, out_summed * scale)


CHAN = ("ring", "pair")


def solution(mesh):
    tm, chan = mesh.shape["tm"], mesh.shape["chan"]
    mesh = jax.sharding.Mesh(mesh.devices.reshape(tm, chan // 2, 2), ("tm", "ring", "pair"))
    placed = (
        P(None, "tm", None),
        P(None, "tm", None),
        P(None, None, None, CHAN),
        P(CHAN, None),
        P(),
    )
    return jax.shard_map(
        local,
        mesh=mesh,
        in_specs=placed,
        out_specs=(P(None, "tm", CHAN), P(None, None, "tm", CHAN), P(CHAN, "tm")),
        check_vma=False,
    )
```

```python
import jax
import jax.numpy as jnp
from jax import lax
from jax.sharding import PartitionSpec as P

DILATION_STEPS = 1024


def shifted(x, axis, by):
    peers = lax.axis_size(axis)
    pairs = [(i, i + by) for i in range(peers) if 0 <= i + by < peers]
    return lax.ppermute(x, axis, pairs)


def contract_rows(left, right):
    return lax.dot_general(
        left, right, (((0,), (0,)), ((), ())), preferred_element_type=jnp.float32
    )


def contract_cols(left, right):
    return lax.dot_general(
        left, right, (((1,), (1,)), ((), ())), preferred_element_type=jnp.float32
    )


def ring_reduce_scatter(x):
    peers = lax.axis_size("ring")
    at = lax.axis_index("ring")
    chunks = x.reshape(peers, x.shape[0] // peers, x.shape[1])
    half = x.shape[1] // 2
    sums = []
    for step, cols in ((1, slice(0, half)), (-1, slice(half, None))):
        own = chunks[:, :, cols]
        pairs = [(i, (i + step) % peers) for i in range(peers)]
        acc = lax.dynamic_index_in_dim(own, (at - step) % peers, 0, keepdims=False)
        for s in range(peers - 1):
            got = lax.ppermute(acc, "ring", pairs)
            acc = got + lax.dynamic_index_in_dim(
                own, (at - step * (s + 2)) % peers, 0, keepdims=False
            )
        sums.append(acc)
    full = jnp.concatenate(sums, axis=1)
    pairs_n = lax.axis_size("pair")
    me = lax.axis_index("pair")
    parts = full.reshape(pairs_n, full.shape[0] // pairs_n, full.shape[1])
    keep = lax.dynamic_index_in_dim(parts, me, 0, keepdims=False)
    give = lax.dynamic_index_in_dim(parts, 1 - me, 0, keepdims=False)
    return keep + lax.ppermute(give, "pair", [(0, 1), (1, 0)])


def local(states, upstream, w_in, w_out, lengths):
    traj, window_extent, width = states.shape
    blocks = w_in.shape[3]
    rows_n = traj * window_extent
    receptive_extent = DILATION_STEPS // window_extent
    rows = states.reshape(rows_n, width)
    w_now = jnp.concatenate([w_in[0, 0], w_in[0, 1]], axis=1)
    w_dil = jnp.concatenate([w_in[1, 0], w_in[1, 1]], axis=1)
    dilated = jnp.dot(rows, w_dil, preferred_element_type=jnp.float32)
    dilated_prior = shifted(
        dilated.reshape(traj, window_extent, 2 * blocks), "tm", receptive_extent
    ).reshape(rows_n, 2 * blocks)
    pre = jnp.dot(rows, w_now, preferred_element_type=jnp.float32) + dilated_prior
    filt = pre[:, :blocks]
    gate = pre[:, blocks:]
    first = lax.axis_index("tm") * window_extent
    positions = first + jnp.arange(window_extent, dtype=jnp.int32)
    valid = positions[None, :] < lengths[:, None]
    grad_rows = jnp.where(valid[:, :, None], upstream, jnp.zeros_like(upstream))
    grad_flat = grad_rows.reshape(rows_n, width)
    tangent = jnp.tanh(filt)
    sigma = jax.nn.sigmoid(gate)
    mixed = (tangent * sigma).astype(jnp.bfloat16)
    dmix = contract_cols(grad_flat, w_out)
    filter_gradient = (dmix * (1.0 - tangent * tangent) * sigma).astype(jnp.bfloat16)
    gate_gradient = (dmix * tangent * sigma * (1.0 - sigma)).astype(jnp.bfloat16)
    branch_grads = jnp.concatenate([filter_gradient, gate_gradient], axis=1)
    later = shifted(
        branch_grads.reshape(traj, window_extent, 2 * blocks), "tm", -receptive_extent
    ).reshape(rows_n, 2 * blocks)
    partial_value = contract_cols(w_now, branch_grads) + contract_cols(w_dil, later)
    summed = ring_reduce_scatter(partial_value)
    share = width // (lax.axis_size("ring") * lax.axis_size("pair"))
    chan_index = lax.axis_index("ring") * lax.axis_size("pair") + lax.axis_index("pair")
    own_rows = lax.dynamic_slice_in_dim(grad_rows, chan_index * share, share, 2)
    summed = summed.reshape(share, traj, window_extent).transpose(1, 2, 0)
    grad_states = (own_rows.astype(jnp.float32) + summed).astype(jnp.bfloat16)
    early = lax.psum_scatter(
        jnp.concatenate(
            [contract_rows(rows, branch_grads), contract_rows(grad_flat, mixed)], axis=1
        ),
        "tm",
        scatter_dimension=0,
        tiled=True,
    )
    early, later_rows, grad_states = lax.optimization_barrier((early, later, grad_states))
    late = lax.psum_scatter(
        contract_rows(rows, later_rows), "tm", scatter_dimension=0, tiled=True
    )
    scale = lax.rsqrt(jnp.sum(lengths.astype(jnp.float32)))
    part = early.shape[0]
    in_summed = jnp.concatenate([early[:, : 2 * blocks], late], axis=1)
    in_summed = in_summed.reshape(part, 2, 2, blocks).transpose(1, 2, 0, 3)
    out_summed = early[:, 2 * blocks :].T
    return (grad_states, in_summed * scale, out_summed * scale)


CHAN = ("ring", "pair")


def solution(mesh):
    tm, chan = mesh.shape["tm"], mesh.shape["chan"]
    mesh = jax.sharding.Mesh(mesh.devices.reshape(tm, chan // 2, 2), ("tm", "ring", "pair"))
    placed = (
        P(None, "tm", None),
        P(None, "tm", None),
        P(None, None, None, CHAN),
        P(CHAN, None),
        P(),
    )
    return jax.shard_map(
        local,
        mesh=mesh,
        in_specs=placed,
        out_specs=(P(None, "tm", CHAN), P(None, None, "tm", CHAN), P(CHAN, "tm")),
        check_vma=False,
    )
```

```python
import jax
import jax.numpy as jnp
from jax import lax
from jax.sharding import PartitionSpec as P

DILATION_STEPS = 1024


TIME = ("tz", "tx", "tc")


def shifted(x, axis, by):
    peers = lax.axis_size(axis[0]) * lax.axis_size(axis[1]) * lax.axis_size(axis[2])
    pairs = [(i, i + by) for i in range(peers) if 0 <= i + by < peers]
    return lax.ppermute(x, axis, pairs)


def contract_rows(left, right):
    return lax.dot_general(
        left, right, (((0,), (0,)), ((), ())), preferred_element_type=jnp.float32
    )


def contract_cols(left, right):
    return lax.dot_general(
        left, right, (((1,), (1,)), ((), ())), preferred_element_type=jnp.float32
    )


def ring_sum(chunks, axis):
    peers = lax.axis_size(axis)
    at = lax.axis_index(axis)
    half = chunks.shape[-1] // 2
    sums = []
    for step, cols in ((1, slice(0, half)), (-1, slice(half, None))):
        own = chunks[..., cols]
        pairs = [(i, (i + step) % peers) for i in range(peers)]
        acc = lax.dynamic_index_in_dim(own, (at - step) % peers, 0, keepdims=False)
        for s in range(peers - 1):
            got = lax.ppermute(acc, axis, pairs)
            acc = got + lax.dynamic_index_in_dim(
                own, (at - step * (s + 2)) % peers, 0, keepdims=False
            )
        sums.append(acc)
    return jnp.concatenate(sums, axis=-1)


def swap_sum(parts, axis):
    me = lax.axis_index(axis)
    keep = lax.dynamic_index_in_dim(parts, me, 0, keepdims=False)
    give = lax.dynamic_index_in_dim(parts, 1 - me, 0, keepdims=False)
    return keep + lax.ppermute(give, axis, [(0, 1), (1, 0)])


def time_reduce_scatter(x):
    outer, mid, inner = (lax.axis_size(a) for a in TIME)
    blocks = x.reshape(outer, mid, inner, x.shape[0] // (outer * mid * inner), x.shape[1])
    blocks = swap_sum(jnp.moveaxis(blocks, 2, 0), TIME[2])
    blocks = ring_sum(blocks, TIME[0])
    return swap_sum(blocks, TIME[1])


def local(states, upstream, w_in, w_out, lengths):
    traj, window_extent, width = states.shape
    blocks = w_in.shape[3]
    rows_n = traj * window_extent
    receptive_extent = DILATION_STEPS // window_extent
    rows = states.reshape(rows_n, width)
    w_now = jnp.concatenate([w_in[0, 0], w_in[0, 1]], axis=1)
    w_dil = jnp.concatenate([w_in[1, 0], w_in[1, 1]], axis=1)
    dilated = jnp.dot(rows, w_dil, preferred_element_type=jnp.float32)
    dilated_prior = shifted(
        dilated.reshape(traj, window_extent, 2 * blocks), TIME, receptive_extent
    ).reshape(rows_n, 2 * blocks)
    pre = jnp.dot(rows, w_now, preferred_element_type=jnp.float32) + dilated_prior
    filt = pre[:, :blocks]
    gate = pre[:, blocks:]
    first = lax.axis_index(TIME) * window_extent
    positions = first + jnp.arange(window_extent, dtype=jnp.int32)
    valid = positions[None, :] < lengths[:, None]
    grad_rows = jnp.where(valid[:, :, None], upstream, jnp.zeros_like(upstream))
    grad_flat = grad_rows.reshape(rows_n, width)
    tangent = jnp.tanh(filt)
    sigma = jax.nn.sigmoid(gate)
    mixed = (tangent * sigma).astype(jnp.bfloat16)
    dmix = contract_cols(grad_flat, w_out)
    filter_gradient = (dmix * (1.0 - tangent * tangent) * sigma).astype(jnp.bfloat16)
    gate_gradient = (dmix * tangent * sigma * (1.0 - sigma)).astype(jnp.bfloat16)
    branch_grads = jnp.concatenate([filter_gradient, gate_gradient], axis=1)
    later = shifted(
        branch_grads.reshape(traj, window_extent, 2 * blocks), TIME, -receptive_extent
    ).reshape(rows_n, 2 * blocks)
    partial_value = contract_cols(w_now, branch_grads) + contract_cols(w_dil, later)
    summed = lax.psum_scatter(partial_value, "chan", scatter_dimension=0, tiled=True)
    share = width // lax.axis_size("chan")
    own_rows = lax.dynamic_slice_in_dim(grad_rows, lax.axis_index("chan") * share, share, 2)
    summed = summed.reshape(share, traj, window_extent).transpose(1, 2, 0)
    grad_states = (own_rows.astype(jnp.float32) + summed).astype(jnp.bfloat16)
    weight_terms = jnp.concatenate(
        [
            contract_rows(rows, branch_grads),
            contract_rows(rows, later),
            contract_rows(grad_flat, mixed),
        ],
        axis=1,
    )
    reduced = time_reduce_scatter(weight_terms)
    scale = lax.rsqrt(jnp.sum(lengths.astype(jnp.float32)))
    part = reduced.shape[0]
    in_summed = reduced[:, : 4 * blocks].reshape(part, 2, 2, blocks).transpose(1, 2, 0, 3)
    out_summed = reduced[:, 4 * blocks :].T
    return (grad_states, in_summed * scale, out_summed * scale)


def solution(mesh):
    tm, chan = mesh.shape["tm"], mesh.shape["chan"]
    mesh = jax.sharding.Mesh(mesh.devices.reshape(tm // 4, 2, 2, chan), TIME + ("chan",))
    placed = (
        P(None, TIME, None),
        P(None, TIME, None),
        P(None, None, None, "chan"),
        P("chan", None),
        P(),
    )
    return jax.shard_map(
        local,
        mesh=mesh,
        in_specs=placed,
        out_specs=(P(None, TIME, "chan"), P(None, None, TIME, "chan"), P("chan", TIME)),
        check_vma=False,
    )
```

```python
import jax
import jax.numpy as jnp
from jax import lax
from jax.sharding import PartitionSpec as P

DILATION_STEPS = 1024


TIME = ("tz", "tx", "tc")


def shifted(x, axis, by):
    peers = lax.axis_size(axis[0]) * lax.axis_size(axis[1]) * lax.axis_size(axis[2])
    pairs = [(i, i + by) for i in range(peers) if 0 <= i + by < peers]
    return lax.ppermute(x, axis, pairs)


def contract_rows(left, right):
    return lax.dot_general(
        left, right, (((0,), (0,)), ((), ())), preferred_element_type=jnp.float32
    )


def contract_cols(left, right):
    return lax.dot_general(
        left, right, (((1,), (1,)), ((), ())), preferred_element_type=jnp.float32
    )


def ring_sum(chunks, axis):
    peers = lax.axis_size(axis)
    at = lax.axis_index(axis)
    sums = []
    for step, half in ((1, 0), (-1, 1)):
        own = chunks[:, half]
        pairs = [(i, (i + step) % peers) for i in range(peers)]
        acc = lax.dynamic_index_in_dim(own, (at - step) % peers, 0, keepdims=False)
        for s in range(peers - 1):
            got = lax.ppermute(acc, axis, pairs)
            acc = got + lax.dynamic_index_in_dim(
                own, (at - step * (s + 2)) % peers, 0, keepdims=False
            )
        sums.append(acc)
    return jnp.stack(sums)


def swap_sum(parts, axis):
    me = lax.axis_index(axis)
    keep = lax.dynamic_index_in_dim(parts, me, 0, keepdims=False)
    give = lax.dynamic_index_in_dim(parts, 1 - me, 0, keepdims=False)
    return keep + lax.ppermute(give, axis, [(0, 1), (1, 0)])


def time_reduce_scatter(left, right):
    outer, mid, inner = (lax.axis_size(a) for a in TIME)
    split = left.reshape(left.shape[0], outer, mid, inner, -1)
    me = lax.axis_index(TIME[2])
    keep = lax.dynamic_index_in_dim(split, me, 3, keepdims=False)
    give = lax.dynamic_index_in_dim(split, 1 - me, 3, keepdims=False)
    keep = contract_rows(keep.reshape(left.shape[0], -1), right)
    give = contract_rows(give.reshape(left.shape[0], -1), right)
    blocks = keep + lax.ppermute(give, TIME[2], [(0, 1), (1, 0)])
    blocks = blocks.reshape(outer, mid, -1, right.shape[1])
    blocks = ring_sum(blocks, TIME[0])
    return swap_sum(blocks, TIME[1])


def local(states, upstream, w_in, w_out, lengths):
    traj, window_extent, width = states.shape
    blocks = w_in.shape[3]
    rows_n = traj * window_extent
    receptive_extent = DILATION_STEPS // window_extent
    rows = states.reshape(rows_n, width)
    w_now = jnp.concatenate([w_in[0, 0], w_in[0, 1]], axis=1)
    w_dil = jnp.concatenate([w_in[1, 0], w_in[1, 1]], axis=1)
    dilated = jnp.dot(rows, w_dil, preferred_element_type=jnp.float32)
    dilated_prior = shifted(
        dilated.reshape(traj, window_extent, 2 * blocks), TIME, receptive_extent
    ).reshape(rows_n, 2 * blocks)
    pre = jnp.dot(rows, w_now, preferred_element_type=jnp.float32) + dilated_prior
    filt = pre[:, :blocks]
    gate = pre[:, blocks:]
    first = lax.axis_index(TIME) * window_extent
    positions = first + jnp.arange(window_extent, dtype=jnp.int32)
    valid = positions[None, :] < lengths[:, None]
    grad_rows = jnp.where(valid[:, :, None], upstream, jnp.zeros_like(upstream))
    grad_flat = grad_rows.reshape(rows_n, width)
    tangent = jnp.tanh(filt)
    sigma = jax.nn.sigmoid(gate)
    mixed = (tangent * sigma).astype(jnp.bfloat16)
    dmix = contract_cols(grad_flat, w_out)
    filter_gradient = (dmix * (1.0 - tangent * tangent) * sigma).astype(jnp.bfloat16)
    gate_gradient = (dmix * tangent * sigma * (1.0 - sigma)).astype(jnp.bfloat16)
    branch_grads = jnp.concatenate([filter_gradient, gate_gradient], axis=1)
    later = shifted(
        branch_grads.reshape(traj, window_extent, 2 * blocks), TIME, -receptive_extent
    ).reshape(rows_n, 2 * blocks)
    partial_value = contract_cols(w_now, branch_grads) + contract_cols(w_dil, later)
    summed = lax.psum_scatter(partial_value, "chan", scatter_dimension=0, tiled=True)
    share = width // lax.axis_size("chan")
    own_rows = lax.dynamic_slice_in_dim(grad_rows, lax.axis_index("chan") * share, share, 2)
    summed = summed.reshape(share, traj, window_extent).transpose(1, 2, 0)
    grad_states = (own_rows.astype(jnp.float32) + summed).astype(jnp.bfloat16)
    left = jnp.concatenate([rows, grad_flat], axis=0)
    zeros = jnp.zeros_like(branch_grads)
    right = jnp.concatenate(
        [
            jnp.concatenate([branch_grads, later, jnp.zeros_like(mixed)], axis=1),
            jnp.concatenate([zeros, zeros, mixed], axis=1),
        ],
        axis=0,
    )
    reduced = time_reduce_scatter(left, right)
    scale = lax.rsqrt(jnp.sum(lengths.astype(jnp.float32)))
    part = reduced.shape[0]
    in_summed = reduced[:, : 4 * blocks].reshape(part, 2, 2, blocks).transpose(1, 2, 0, 3)
    out_summed = reduced[:, 4 * blocks :].T
    return (grad_states, in_summed * scale, out_summed * scale)


def solution(mesh):
    tm, chan = mesh.shape["tm"], mesh.shape["chan"]
    mesh = jax.sharding.Mesh(mesh.devices.reshape(tm // 4, 2, 2, chan), TIME + ("chan",))
    placed = (
        P(None, TIME, None),
        P(None, TIME, None),
        P(None, None, None, "chan"),
        P("chan", None),
        P(),
    )
    return jax.shard_map(
        local,
        mesh=mesh,
        in_specs=placed,
        out_specs=(P(None, TIME, "chan"), P(None, None, TIME, "chan"), P("chan", TIME)),
        check_vma=False,
    )
```

```python
import jax
import jax.numpy as jnp
from jax import lax
from jax.sharding import PartitionSpec as P

DILATION_STEPS = 1024


TIME = ("tz", "tx", "tc")
CHAN = ("cy", "cx")


def shifted(x, axis, by):
    peers = lax.axis_size(axis[0]) * lax.axis_size(axis[1]) * lax.axis_size(axis[2])
    pairs = [(i, i + by) for i in range(peers) if 0 <= i + by < peers]
    return lax.ppermute(x, axis, pairs)


def contract_rows(left, right):
    return lax.dot_general(
        left, right, (((0,), (0,)), ((), ())), preferred_element_type=jnp.float32
    )


def contract_cols(left, right):
    return lax.dot_general(
        left, right, (((1,), (1,)), ((), ())), preferred_element_type=jnp.float32
    )


def ring_sum(chunks, axis):
    peers = lax.axis_size(axis)
    at = lax.axis_index(axis)
    half = chunks.shape[-1] // 2
    sums = []
    for step, cols in ((1, slice(0, half)), (-1, slice(half, None))):
        own = chunks[..., cols]
        pairs = [(i, (i + step) % peers) for i in range(peers)]
        acc = lax.dynamic_index_in_dim(own, (at - step) % peers, 0, keepdims=False)
        for s in range(peers - 1):
            got = lax.ppermute(acc, axis, pairs)
            acc = got + lax.dynamic_index_in_dim(
                own, (at - step * (s + 2)) % peers, 0, keepdims=False
            )
        sums.append(acc)
    return jnp.concatenate(sums, axis=-1)


def swap_sum(parts, axis):
    me = lax.axis_index(axis)
    keep = lax.dynamic_index_in_dim(parts, me, 0, keepdims=False)
    give = lax.dynamic_index_in_dim(parts, 1 - me, 0, keepdims=False)
    return keep + lax.ppermute(give, axis, [(0, 1), (1, 0)])


def chan_ring_reduce_scatter(x):
    peers = lax.axis_size("cy")
    at = lax.axis_index("cy")
    chunks = x.reshape(peers, x.shape[0] // peers, x.shape[1])
    half = x.shape[1] // 2
    sums = []
    for step, cols in ((1, slice(0, half)), (-1, slice(half, None))):
        own = chunks[:, :, cols]
        pairs = [(i, (i + step) % peers) for i in range(peers)]
        acc = lax.dynamic_index_in_dim(own, (at - step) % peers, 0, keepdims=False)
        for s in range(peers - 1):
            got = lax.ppermute(acc, "cy", pairs)
            acc = got + lax.dynamic_index_in_dim(
                own, (at - step * (s + 2)) % peers, 0, keepdims=False
            )
        sums.append(acc)
    full = jnp.concatenate(sums, axis=1)
    return swap_sum(full.reshape(2, full.shape[0] // 2, full.shape[1]), "cx")


def time_reduce_scatter(x):
    outer, mid, inner = (lax.axis_size(a) for a in TIME)
    blocks = x.reshape(outer, mid, inner, x.shape[0] // (outer * mid * inner), x.shape[1])
    blocks = swap_sum(jnp.moveaxis(blocks, 2, 0), TIME[2])
    blocks = ring_sum(blocks, TIME[0])
    return swap_sum(blocks, TIME[1])


def local(states, upstream, w_in, w_out, lengths):
    traj, window_extent, width = states.shape
    blocks = w_in.shape[3]
    rows_n = traj * window_extent
    receptive_extent = DILATION_STEPS // window_extent
    rows = states.reshape(rows_n, width)
    w_now = jnp.concatenate([w_in[0, 0], w_in[0, 1]], axis=1)
    w_dil = jnp.concatenate([w_in[1, 0], w_in[1, 1]], axis=1)
    dilated = jnp.dot(rows, w_dil, preferred_element_type=jnp.float32)
    dilated_prior = shifted(
        dilated.reshape(traj, window_extent, 2 * blocks), TIME, receptive_extent
    ).reshape(rows_n, 2 * blocks)
    pre = jnp.dot(rows, w_now, preferred_element_type=jnp.float32) + dilated_prior
    filt = pre[:, :blocks]
    gate = pre[:, blocks:]
    first = lax.axis_index(TIME) * window_extent
    positions = first + jnp.arange(window_extent, dtype=jnp.int32)
    valid = positions[None, :] < lengths[:, None]
    grad_rows = jnp.where(valid[:, :, None], upstream, jnp.zeros_like(upstream))
    grad_flat = grad_rows.reshape(rows_n, width)
    tangent = jnp.tanh(filt)
    sigma = jax.nn.sigmoid(gate)
    mixed = (tangent * sigma).astype(jnp.bfloat16)
    dmix = contract_cols(grad_flat, w_out)
    filter_gradient = (dmix * (1.0 - tangent * tangent) * sigma).astype(jnp.bfloat16)
    gate_gradient = (dmix * tangent * sigma * (1.0 - sigma)).astype(jnp.bfloat16)
    branch_grads = jnp.concatenate([filter_gradient, gate_gradient], axis=1)
    later = shifted(
        branch_grads.reshape(traj, window_extent, 2 * blocks), TIME, -receptive_extent
    ).reshape(rows_n, 2 * blocks)
    partial_value = contract_cols(w_now, branch_grads) + contract_cols(w_dil, later)
    cut = partial_value.shape[1] // 2
    summed = jnp.concatenate(
        [
            lax.psum_scatter(partial_value[:, :cut], CHAN, scatter_dimension=0, tiled=True),
            chan_ring_reduce_scatter(partial_value[:, cut:]),
        ],
        axis=1,
    )
    share = width // (lax.axis_size("cy") * lax.axis_size("cx"))
    own_rows = lax.dynamic_slice_in_dim(grad_rows, lax.axis_index(CHAN) * share, share, 2)
    summed = summed.reshape(share, traj, window_extent).transpose(1, 2, 0)
    grad_states = (own_rows.astype(jnp.float32) + summed).astype(jnp.bfloat16)
    weight_terms = jnp.concatenate(
        [
            contract_rows(rows, branch_grads),
            contract_rows(rows, later),
            contract_rows(grad_flat, mixed),
        ],
        axis=1,
    )
    reduced = time_reduce_scatter(weight_terms)
    scale = lax.rsqrt(jnp.sum(lengths.astype(jnp.float32)))
    part = reduced.shape[0]
    in_summed = reduced[:, : 4 * blocks].reshape(part, 2, 2, blocks).transpose(1, 2, 0, 3)
    out_summed = reduced[:, 4 * blocks :].T
    return (grad_states, in_summed * scale, out_summed * scale)


def solution(mesh):
    tm, chan = mesh.shape["tm"], mesh.shape["chan"]
    mesh = jax.sharding.Mesh(mesh.devices.reshape(tm // 4, 2, 2, chan // 2, 2), TIME + CHAN)
    placed = (
        P(None, TIME, None),
        P(None, TIME, None),
        P(None, None, None, CHAN),
        P(CHAN, None),
        P(),
    )
    return jax.shard_map(
        local,
        mesh=mesh,
        in_specs=placed,
        out_specs=(P(None, TIME, CHAN), P(None, None, TIME, CHAN), P(CHAN, TIME)),
        check_vma=False,
    )
```

```python
import jax
import jax.numpy as jnp
from jax import lax
from jax.sharding import PartitionSpec as P

DILATION_STEPS = 1024


TIME = ("tz", "tx", "tc")
CHAN = ("cy", "cx")


def shifted(x, axis, by):
    peers = lax.axis_size(axis[0]) * lax.axis_size(axis[1]) * lax.axis_size(axis[2])
    pairs = [(i, i + by) for i in range(peers) if 0 <= i + by < peers]
    return lax.ppermute(x, axis, pairs)


def contract_rows(left, right):
    return lax.dot_general(
        left, right, (((0,), (0,)), ((), ())), preferred_element_type=jnp.float32
    )


def contract_cols(left, right):
    return lax.dot_general(
        left, right, (((1,), (1,)), ((), ())), preferred_element_type=jnp.float32
    )


def ring_sum(chunks, axis):
    peers = lax.axis_size(axis)
    at = lax.axis_index(axis)
    half = chunks.shape[-1] // 2
    sums = []
    for step, cols in ((1, slice(0, half)), (-1, slice(half, None))):
        own = chunks[..., cols]
        pairs = [(i, (i + step) % peers) for i in range(peers)]
        acc = lax.dynamic_index_in_dim(own, (at - step) % peers, 0, keepdims=False)
        for s in range(peers - 1):
            got = lax.ppermute(acc, axis, pairs)
            acc = got + lax.dynamic_index_in_dim(
                own, (at - step * (s + 2)) % peers, 0, keepdims=False
            )
        sums.append(acc)
    return jnp.concatenate(sums, axis=-1)


def swap_sum(parts, axis):
    me = lax.axis_index(axis)
    keep = lax.dynamic_index_in_dim(parts, me, 0, keepdims=False)
    give = lax.dynamic_index_in_dim(parts, 1 - me, 0, keepdims=False)
    return keep + lax.ppermute(give, axis, [(0, 1), (1, 0)])


def chan_ring_reduce_scatter(x):
    peers = lax.axis_size("cy")
    at = lax.axis_index("cy")
    chunks = x.reshape(peers, x.shape[0] // peers, x.shape[1])
    half = x.shape[1] // 2
    sums = []
    for step, cols in ((1, slice(0, half)), (-1, slice(half, None))):
        own = chunks[:, :, cols]
        pairs = [(i, (i + step) % peers) for i in range(peers)]
        acc = lax.dynamic_index_in_dim(own, (at - step) % peers, 0, keepdims=False)
        for s in range(peers - 1):
            got = lax.ppermute(acc, "cy", pairs)
            acc = got + lax.dynamic_index_in_dim(
                own, (at - step * (s + 2)) % peers, 0, keepdims=False
            )
        sums.append(acc)
    full = jnp.concatenate(sums, axis=1)
    return swap_sum(full.reshape(2, full.shape[0] // 2, full.shape[1]), "cx")


def time_reduce_scatter(x):
    outer, mid, inner = (lax.axis_size(a) for a in TIME)
    blocks = x.reshape(outer, mid, inner, x.shape[0] // (outer * mid * inner), x.shape[1])
    blocks = swap_sum(jnp.moveaxis(blocks, 2, 0), TIME[2])
    blocks = ring_sum(blocks, TIME[0])
    return swap_sum(blocks, TIME[1])


def local(states, upstream, w_in, w_out, lengths):
    traj, window_extent, width = states.shape
    blocks = w_in.shape[3]
    rows_n = traj * window_extent
    receptive_extent = DILATION_STEPS // window_extent
    rows = states.reshape(rows_n, width)
    w_now = jnp.concatenate([w_in[0, 0], w_in[0, 1]], axis=1)
    w_dil = jnp.concatenate([w_in[1, 0], w_in[1, 1]], axis=1)
    dilated = jnp.dot(rows, w_dil, preferred_element_type=jnp.float32)
    dilated_prior = shifted(
        dilated.reshape(traj, window_extent, 2 * blocks), TIME, receptive_extent
    ).reshape(rows_n, 2 * blocks)
    pre = jnp.dot(rows, w_now, preferred_element_type=jnp.float32) + dilated_prior
    filt = pre[:, :blocks]
    gate = pre[:, blocks:]
    first = lax.axis_index(TIME) * window_extent
    positions = first + jnp.arange(window_extent, dtype=jnp.int32)
    valid = positions[None, :] < lengths[:, None]
    grad_rows = jnp.where(valid[:, :, None], upstream, jnp.zeros_like(upstream))
    grad_flat = grad_rows.reshape(rows_n, width)
    tangent = jnp.tanh(filt)
    sigma = jax.nn.sigmoid(gate)
    mixed = (tangent * sigma).astype(jnp.bfloat16)
    dmix = contract_cols(grad_flat, w_out)
    filter_gradient = (dmix * (1.0 - tangent * tangent) * sigma).astype(jnp.bfloat16)
    gate_gradient = (dmix * tangent * sigma * (1.0 - sigma)).astype(jnp.bfloat16)
    branch_grads = jnp.concatenate([filter_gradient, gate_gradient], axis=1)
    later = shifted(
        branch_grads.reshape(traj, window_extent, 2 * blocks), TIME, -receptive_extent
    ).reshape(rows_n, 2 * blocks)
    partial_value = contract_cols(w_now, branch_grads) + contract_cols(w_dil, later)
    cut = partial_value.shape[1] * 3 // 4
    summed = jnp.concatenate(
        [
            lax.psum_scatter(partial_value[:, :cut], CHAN, scatter_dimension=0, tiled=True),
            chan_ring_reduce_scatter(partial_value[:, cut:]),
        ],
        axis=1,
    )
    share = width // (lax.axis_size("cy") * lax.axis_size("cx"))
    own_rows = lax.dynamic_slice_in_dim(grad_rows, lax.axis_index(CHAN) * share, share, 2)
    summed = summed.reshape(share, traj, window_extent).transpose(1, 2, 0)
    grad_states = (own_rows.astype(jnp.float32) + summed).astype(jnp.bfloat16)
    weight_terms = jnp.concatenate(
        [
            contract_rows(rows, branch_grads),
            contract_rows(rows, later),
            contract_rows(grad_flat, mixed),
        ],
        axis=1,
    )
    reduced = time_reduce_scatter(weight_terms)
    scale = lax.rsqrt(jnp.sum(lengths.astype(jnp.float32)))
    part = reduced.shape[0]
    in_summed = reduced[:, : 4 * blocks].reshape(part, 2, 2, blocks).transpose(1, 2, 0, 3)
    out_summed = reduced[:, 4 * blocks :].T
    return (grad_states, in_summed * scale, out_summed * scale)


def solution(mesh):
    tm, chan = mesh.shape["tm"], mesh.shape["chan"]
    mesh = jax.sharding.Mesh(mesh.devices.reshape(tm // 4, 2, 2, chan // 2, 2), TIME + CHAN)
    placed = (
        P(None, TIME, None),
        P(None, TIME, None),
        P(None, None, None, CHAN),
        P(CHAN, None),
        P(),
    )
    return jax.shard_map(
        local,
        mesh=mesh,
        in_specs=placed,
        out_specs=(P(None, TIME, CHAN), P(None, None, TIME, CHAN), P(CHAN, TIME)),
        check_vma=False,
    )
```

```python
import jax
import jax.numpy as jnp
from jax import lax
from jax.sharding import PartitionSpec as P

DILATION_STEPS = 1024


TIME = ("tz", "tx", "tc")
CHAN = ("cy", "cx")


def shifted(x, axis, by):
    peers = lax.axis_size(axis[0]) * lax.axis_size(axis[1]) * lax.axis_size(axis[2])
    pairs = [(i, i + by) for i in range(peers) if 0 <= i + by < peers]
    return lax.ppermute(x, axis, pairs)


def contract_rows(left, right):
    return lax.dot_general(
        left, right, (((0,), (0,)), ((), ())), preferred_element_type=jnp.float32
    )


def contract_cols(left, right):
    return lax.dot_general(
        left, right, (((1,), (1,)), ((), ())), preferred_element_type=jnp.float32
    )


def ring_sum(chunks, axis):
    peers = lax.axis_size(axis)
    at = lax.axis_index(axis)
    sums = []
    for step, half in ((1, 0), (-1, 1)):
        own = chunks[:, half]
        pairs = [(i, (i + step) % peers) for i in range(peers)]
        acc = lax.dynamic_index_in_dim(own, (at - step) % peers, 0, keepdims=False)
        for s in range(peers - 1):
            got = lax.ppermute(acc, axis, pairs)
            acc = got + lax.dynamic_index_in_dim(
                own, (at - step * (s + 2)) % peers, 0, keepdims=False
            )
        sums.append(acc)
    return jnp.stack(sums)


def swap_sum(parts, axis):
    me = lax.axis_index(axis)
    keep = lax.dynamic_index_in_dim(parts, me, 0, keepdims=False)
    give = lax.dynamic_index_in_dim(parts, 1 - me, 0, keepdims=False)
    return keep + lax.ppermute(give, axis, [(0, 1), (1, 0)])


def chan_ring_reduce_scatter(x):
    peers = lax.axis_size("cy")
    at = lax.axis_index("cy")
    chunks = x.reshape(peers, x.shape[0] // peers, x.shape[1])
    half = x.shape[1] // 2
    sums = []
    for step, cols in ((1, slice(0, half)), (-1, slice(half, None))):
        own = chunks[:, :, cols]
        pairs = [(i, (i + step) % peers) for i in range(peers)]
        acc = lax.dynamic_index_in_dim(own, (at - step) % peers, 0, keepdims=False)
        for s in range(peers - 1):
            got = lax.ppermute(acc, "cy", pairs)
            acc = got + lax.dynamic_index_in_dim(
                own, (at - step * (s + 2)) % peers, 0, keepdims=False
            )
        sums.append(acc)
    full = jnp.concatenate(sums, axis=1)
    return swap_sum(full.reshape(2, full.shape[0] // 2, full.shape[1]), "cx")


def time_reduce_scatter(x):
    outer, mid, inner = (lax.axis_size(a) for a in TIME)
    blocks = x.reshape(outer, mid, inner, x.shape[0] // (outer * mid * inner), x.shape[1])
    blocks = swap_sum(jnp.moveaxis(blocks, 2, 0), TIME[2])
    blocks = ring_sum(blocks, TIME[0])
    return swap_sum(blocks, TIME[1])


def local(states, upstream, w_in, w_out, lengths):
    traj, window_extent, width = states.shape
    blocks = w_in.shape[3]
    rows_n = traj * window_extent
    receptive_extent = DILATION_STEPS // window_extent
    rows = states.reshape(rows_n, width)
    w_now = jnp.concatenate([w_in[0, 0], w_in[0, 1]], axis=1)
    w_dil = jnp.concatenate([w_in[1, 0], w_in[1, 1]], axis=1)
    dilated = jnp.dot(rows, w_dil, preferred_element_type=jnp.float32)
    dilated_prior = shifted(
        dilated.reshape(traj, window_extent, 2 * blocks), TIME, receptive_extent
    ).reshape(rows_n, 2 * blocks)
    pre = jnp.dot(rows, w_now, preferred_element_type=jnp.float32) + dilated_prior
    filt = pre[:, :blocks]
    gate = pre[:, blocks:]
    first = lax.axis_index(TIME) * window_extent
    positions = first + jnp.arange(window_extent, dtype=jnp.int32)
    valid = positions[None, :] < lengths[:, None]
    grad_rows = jnp.where(valid[:, :, None], upstream, jnp.zeros_like(upstream))
    grad_flat = grad_rows.reshape(rows_n, width)
    tangent = jnp.tanh(filt)
    sigma = jax.nn.sigmoid(gate)
    mixed = (tangent * sigma).astype(jnp.bfloat16)
    dmix = contract_cols(grad_flat, w_out)
    filter_gradient = (dmix * (1.0 - tangent * tangent) * sigma).astype(jnp.bfloat16)
    gate_gradient = (dmix * tangent * sigma * (1.0 - sigma)).astype(jnp.bfloat16)
    branch_grads = jnp.concatenate([filter_gradient, gate_gradient], axis=1)
    later = shifted(
        branch_grads.reshape(traj, window_extent, 2 * blocks), TIME, -receptive_extent
    ).reshape(rows_n, 2 * blocks)
    partial_value = contract_cols(w_now, branch_grads) + contract_cols(w_dil, later)
    cut = partial_value.shape[1] // 2
    summed = jnp.concatenate(
        [
            lax.psum_scatter(partial_value[:, :cut], CHAN, scatter_dimension=0, tiled=True),
            chan_ring_reduce_scatter(partial_value[:, cut:]),
        ],
        axis=1,
    )
    share = width // (lax.axis_size("cy") * lax.axis_size("cx"))
    own_rows = lax.dynamic_slice_in_dim(grad_rows, lax.axis_index(CHAN) * share, share, 2)
    summed = summed.reshape(share, traj, window_extent).transpose(1, 2, 0)
    grad_states = (own_rows.astype(jnp.float32) + summed).astype(jnp.bfloat16)
    weight_terms = jnp.concatenate(
        [
            contract_rows(rows, branch_grads),
            contract_rows(rows, later),
            contract_rows(grad_flat, mixed),
        ],
        axis=1,
    )
    reduced = time_reduce_scatter(weight_terms)
    scale = lax.rsqrt(jnp.sum(lengths.astype(jnp.float32)))
    part = reduced.shape[0]
    in_summed = reduced[:, : 4 * blocks].reshape(part, 2, 2, blocks).transpose(1, 2, 0, 3)
    out_summed = reduced[:, 4 * blocks :].T
    return (grad_states, in_summed * scale, out_summed * scale)


def solution(mesh):
    tm, chan = mesh.shape["tm"], mesh.shape["chan"]
    mesh = jax.sharding.Mesh(mesh.devices.reshape(tm // 4, 2, 2, chan // 2, 2), TIME + CHAN)
    placed = (
        P(None, TIME, None),
        P(None, TIME, None),
        P(None, None, None, CHAN),
        P(CHAN, None),
        P(),
    )
    return jax.shard_map(
        local,
        mesh=mesh,
        in_specs=placed,
        out_specs=(P(None, TIME, CHAN), P(None, None, TIME, CHAN), P(CHAN, TIME)),
        check_vma=False,
    )
```

```python
import jax
import jax.numpy as jnp
from jax import lax
from jax.sharding import PartitionSpec as P

DILATION_STEPS = 1024


TIME = ("tz", "tx", "tc")
CHAN = ("cy", "cx")


def shifted(x, axis, by):
    peers = lax.axis_size(axis[0]) * lax.axis_size(axis[1]) * lax.axis_size(axis[2])
    pairs = [(i, i + by) for i in range(peers) if 0 <= i + by < peers]
    return lax.ppermute(x, axis, pairs)


def contract_rows(left, right):
    return lax.dot_general(
        left, right, (((0,), (0,)), ((), ())), preferred_element_type=jnp.float32
    )


def contract_cols(left, right):
    return lax.dot_general(
        left, right, (((1,), (1,)), ((), ())), preferred_element_type=jnp.float32
    )


def ring_sum(chunks, axis):
    peers = lax.axis_size(axis)
    at = lax.axis_index(axis)
    half = chunks.shape[-1] // 2
    sums = []
    for step, cols in ((1, slice(0, half)), (-1, slice(half, None))):
        own = chunks[..., cols]
        pairs = [(i, (i + step) % peers) for i in range(peers)]
        acc = lax.dynamic_index_in_dim(own, (at - step) % peers, 0, keepdims=False)
        for s in range(peers - 1):
            got = lax.ppermute(acc, axis, pairs)
            acc = got + lax.dynamic_index_in_dim(
                own, (at - step * (s + 2)) % peers, 0, keepdims=False
            )
        sums.append(acc)
    return jnp.concatenate(sums, axis=-1)


def swap_sum(parts, axis):
    me = lax.axis_index(axis)
    keep = lax.dynamic_index_in_dim(parts, me, 0, keepdims=False)
    give = lax.dynamic_index_in_dim(parts, 1 - me, 0, keepdims=False)
    return keep + lax.ppermute(give, axis, [(0, 1), (1, 0)])


def chan_ring_reduce_scatter(x):
    peers = lax.axis_size("cy")
    at = lax.axis_index("cy")
    chunks = x.reshape(peers, x.shape[0] // peers, x.shape[1])
    half = x.shape[1] // 2
    sums = []
    for step, cols in ((1, slice(0, half)), (-1, slice(half, None))):
        own = chunks[:, :, cols]
        pairs = [(i, (i + step) % peers) for i in range(peers)]
        acc = lax.dynamic_index_in_dim(own, (at - step) % peers, 0, keepdims=False)
        for s in range(peers - 1):
            got = lax.ppermute(acc, "cy", pairs)
            acc = got + lax.dynamic_index_in_dim(
                own, (at - step * (s + 2)) % peers, 0, keepdims=False
            )
        sums.append(acc)
    full = jnp.concatenate(sums, axis=1)
    return swap_sum(full.reshape(2, full.shape[0] // 2, full.shape[1]), "cx")


def time_reduce_scatter(x):
    outer, mid, inner = (lax.axis_size(a) for a in TIME)
    blocks = x.reshape(outer, mid, inner, x.shape[0] // (outer * mid * inner), x.shape[1])
    blocks = swap_sum(jnp.moveaxis(blocks, 2, 0), TIME[2])
    blocks = ring_sum(blocks, TIME[0])
    return swap_sum(blocks, TIME[1])


def local(states, upstream, w_in, w_out, lengths):
    traj, window_extent, width = states.shape
    blocks = w_in.shape[3]
    rows_n = traj * window_extent
    receptive_extent = DILATION_STEPS // window_extent
    rows = states.reshape(rows_n, width)
    w_now = jnp.concatenate([w_in[0, 0], w_in[0, 1]], axis=1)
    w_dil = jnp.concatenate([w_in[1, 0], w_in[1, 1]], axis=1)
    dilated = jnp.dot(rows, w_dil, preferred_element_type=jnp.float32)
    dilated_prior = shifted(
        dilated.reshape(traj, window_extent, 2 * blocks), TIME, receptive_extent
    ).reshape(rows_n, 2 * blocks)
    pre = jnp.dot(rows, w_now, preferred_element_type=jnp.float32) + dilated_prior
    filt = pre[:, :blocks]
    gate = pre[:, blocks:]
    first = lax.axis_index(TIME) * window_extent
    positions = first + jnp.arange(window_extent, dtype=jnp.int32)
    valid = positions[None, :] < lengths[:, None]
    grad_rows = jnp.where(valid[:, :, None], upstream, jnp.zeros_like(upstream))
    grad_flat = grad_rows.reshape(rows_n, width)
    tangent = jnp.tanh(filt)
    sigma = jax.nn.sigmoid(gate)
    mixed = (tangent * sigma).astype(jnp.bfloat16)
    dmix = contract_cols(grad_flat, w_out)
    filter_gradient = (dmix * (1.0 - tangent * tangent) * sigma).astype(jnp.bfloat16)
    gate_gradient = (dmix * tangent * sigma * (1.0 - sigma)).astype(jnp.bfloat16)
    branch_grads = jnp.concatenate([filter_gradient, gate_gradient], axis=1)
    later = shifted(
        branch_grads.reshape(traj, window_extent, 2 * blocks), TIME, -receptive_extent
    ).reshape(rows_n, 2 * blocks)
    partial_value = contract_cols(w_now, branch_grads) + contract_cols(w_dil, later)
    cut = partial_value.shape[1] // 2
    summed = jnp.concatenate(
        [
            lax.psum_scatter(partial_value[:, :cut], CHAN, scatter_dimension=0, tiled=True),
            chan_ring_reduce_scatter(partial_value[:, cut:]),
        ],
        axis=1,
    )
    share = width // (lax.axis_size("cy") * lax.axis_size("cx"))
    own_rows = lax.dynamic_slice_in_dim(grad_rows, lax.axis_index(CHAN) * share, share, 2)
    summed = summed.reshape(share, traj, window_extent).transpose(1, 2, 0)
    grad_states = (own_rows.astype(jnp.float32) + summed).astype(jnp.bfloat16)
    zeros = jnp.zeros_like(branch_grads)
    right = jnp.concatenate(
        [
            jnp.concatenate([branch_grads, later, jnp.zeros_like(mixed)], axis=1),
            jnp.concatenate([zeros, zeros, mixed], axis=1),
        ],
        axis=0,
    )
    weight_terms = contract_rows(jnp.concatenate([rows, grad_flat], axis=0), right)
    reduced = time_reduce_scatter(weight_terms)
    scale = lax.rsqrt(jnp.sum(lengths.astype(jnp.float32)))
    part = reduced.shape[0]
    in_summed = reduced[:, : 4 * blocks].reshape(part, 2, 2, blocks).transpose(1, 2, 0, 3)
    out_summed = reduced[:, 4 * blocks :].T
    return (grad_states, in_summed * scale, out_summed * scale)


def solution(mesh):
    tm, chan = mesh.shape["tm"], mesh.shape["chan"]
    mesh = jax.sharding.Mesh(mesh.devices.reshape(tm // 4, 2, 2, chan // 2, 2), TIME + CHAN)
    placed = (
        P(None, TIME, None),
        P(None, TIME, None),
        P(None, None, None, CHAN),
        P(CHAN, None),
        P(),
    )
    return jax.shard_map(
        local,
        mesh=mesh,
        in_specs=placed,
        out_specs=(P(None, TIME, CHAN), P(None, None, TIME, CHAN), P(CHAN, TIME)),
        check_vma=False,
    )
```

```python
import jax
import jax.numpy as jnp
from jax import lax
from jax.sharding import PartitionSpec as P

DILATION_STEPS = 1024


TIME = ("tz", "tx", "tc")
CHAN = ("cy", "cx")


def shifted(x, axis, by):
    peers = lax.axis_size(axis[0]) * lax.axis_size(axis[1]) * lax.axis_size(axis[2])
    pairs = [(i, i + by) for i in range(peers) if 0 <= i + by < peers]
    return lax.ppermute(x, axis, pairs)


def contract_rows(left, right):
    return lax.dot_general(
        left, right, (((0,), (0,)), ((), ())), preferred_element_type=jnp.float32
    )


def contract_cols(left, right):
    return lax.dot_general(
        left, right, (((1,), (1,)), ((), ())), preferred_element_type=jnp.float32
    )


def ring_sum(chunks, axis):
    peers = lax.axis_size(axis)
    at = lax.axis_index(axis)
    half = chunks.shape[-1] // 2
    sums = []
    for step, cols in ((1, slice(0, half)), (-1, slice(half, None))):
        own = chunks[..., cols]
        pairs = [(i, (i + step) % peers) for i in range(peers)]
        acc = lax.dynamic_index_in_dim(own, (at - step) % peers, 0, keepdims=False)
        for s in range(peers - 1):
            got = lax.ppermute(acc, axis, pairs)
            acc = got + lax.dynamic_index_in_dim(
                own, (at - step * (s + 2)) % peers, 0, keepdims=False
            )
        sums.append(acc)
    return jnp.concatenate(sums, axis=-1)


def swap_sum(parts, axis):
    me = lax.axis_index(axis)
    keep = lax.dynamic_index_in_dim(parts, me, 0, keepdims=False)
    give = lax.dynamic_index_in_dim(parts, 1 - me, 0, keepdims=False)
    return keep + lax.ppermute(give, axis, [(0, 1), (1, 0)])


def chan_ring_reduce_scatter(x):
    peers = lax.axis_size("cy")
    at = lax.axis_index("cy")
    chunks = x.reshape(peers, x.shape[0] // peers, x.shape[1])
    half = x.shape[1] // 2
    sums = []
    for step, cols in ((1, slice(0, half)), (-1, slice(half, None))):
        own = chunks[:, :, cols]
        pairs = [(i, (i + step) % peers) for i in range(peers)]
        acc = lax.dynamic_index_in_dim(own, (at - step) % peers, 0, keepdims=False)
        for s in range(peers - 1):
            got = lax.ppermute(acc, "cy", pairs)
            acc = got + lax.dynamic_index_in_dim(
                own, (at - step * (s + 2)) % peers, 0, keepdims=False
            )
        sums.append(acc)
    full = jnp.concatenate(sums, axis=1)
    return swap_sum(full.reshape(2, full.shape[0] // 2, full.shape[1]), "cx")


def time_reduce_scatter(left, right):
    outer, mid, inner = (lax.axis_size(a) for a in TIME)
    split = left.reshape(left.shape[0], outer, mid, inner, -1)
    me = lax.axis_index(TIME[2])
    pair = [(0, 1), (1, 0)]
    keep = lax.dynamic_index_in_dim(split, me, 3, keepdims=False).reshape(left.shape[0], -1)
    give = lax.dynamic_index_in_dim(split, 1 - me, 3, keepdims=False).reshape(left.shape[0], -1)
    both_left = jnp.concatenate([keep, lax.ppermute(give, TIME[2], pair)], axis=0)
    both_right = jnp.concatenate([right, lax.ppermute(right, TIME[2], pair)], axis=0)
    blocks = contract_rows(both_left, both_right).reshape(outer, mid, -1, right.shape[1])
    blocks = ring_sum(blocks, TIME[0])
    return swap_sum(blocks, TIME[1])


def local(states, upstream, w_in, w_out, lengths):
    traj, window_extent, width = states.shape
    blocks = w_in.shape[3]
    rows_n = traj * window_extent
    receptive_extent = DILATION_STEPS // window_extent
    rows = states.reshape(rows_n, width)
    w_now = jnp.concatenate([w_in[0, 0], w_in[0, 1]], axis=1)
    w_dil = jnp.concatenate([w_in[1, 0], w_in[1, 1]], axis=1)
    dilated = jnp.dot(rows, w_dil, preferred_element_type=jnp.float32)
    dilated_prior = shifted(
        dilated.reshape(traj, window_extent, 2 * blocks), TIME, receptive_extent
    ).reshape(rows_n, 2 * blocks)
    pre = jnp.dot(rows, w_now, preferred_element_type=jnp.float32) + dilated_prior
    filt = pre[:, :blocks]
    gate = pre[:, blocks:]
    first = lax.axis_index(TIME) * window_extent
    positions = first + jnp.arange(window_extent, dtype=jnp.int32)
    valid = positions[None, :] < lengths[:, None]
    grad_rows = jnp.where(valid[:, :, None], upstream, jnp.zeros_like(upstream))
    grad_flat = grad_rows.reshape(rows_n, width)
    tangent = jnp.tanh(filt)
    sigma = jax.nn.sigmoid(gate)
    mixed = (tangent * sigma).astype(jnp.bfloat16)
    dmix = contract_cols(grad_flat, w_out)
    filter_gradient = (dmix * (1.0 - tangent * tangent) * sigma).astype(jnp.bfloat16)
    gate_gradient = (dmix * tangent * sigma * (1.0 - sigma)).astype(jnp.bfloat16)
    branch_grads = jnp.concatenate([filter_gradient, gate_gradient], axis=1)
    later = shifted(
        branch_grads.reshape(traj, window_extent, 2 * blocks), TIME, -receptive_extent
    ).reshape(rows_n, 2 * blocks)
    partial_value = contract_cols(w_now, branch_grads) + contract_cols(w_dil, later)
    cut = partial_value.shape[1] // 2
    summed = jnp.concatenate(
        [
            lax.psum_scatter(partial_value[:, :cut], CHAN, scatter_dimension=0, tiled=True),
            chan_ring_reduce_scatter(partial_value[:, cut:]),
        ],
        axis=1,
    )
    share = width // (lax.axis_size("cy") * lax.axis_size("cx"))
    own_rows = lax.dynamic_slice_in_dim(grad_rows, lax.axis_index(CHAN) * share, share, 2)
    summed = summed.reshape(share, traj, window_extent).transpose(1, 2, 0)
    grad_states = (own_rows.astype(jnp.float32) + summed).astype(jnp.bfloat16)
    zeros = jnp.zeros_like(branch_grads)
    right = jnp.concatenate(
        [
            jnp.concatenate([branch_grads, later, jnp.zeros_like(mixed)], axis=1),
            jnp.concatenate([zeros, zeros, mixed], axis=1),
        ],
        axis=0,
    )
    reduced = time_reduce_scatter(jnp.concatenate([rows, grad_flat], axis=0), right)
    scale = lax.rsqrt(jnp.sum(lengths.astype(jnp.float32)))
    part = reduced.shape[0]
    in_summed = reduced[:, : 4 * blocks].reshape(part, 2, 2, blocks).transpose(1, 2, 0, 3)
    out_summed = reduced[:, 4 * blocks :].T
    return (grad_states, in_summed * scale, out_summed * scale)


def solution(mesh):
    tm, chan = mesh.shape["tm"], mesh.shape["chan"]
    mesh = jax.sharding.Mesh(mesh.devices.reshape(tm // 4, 2, 2, chan // 2, 2), TIME + CHAN)
    placed = (
        P(None, TIME, None),
        P(None, TIME, None),
        P(None, None, None, CHAN),
        P(CHAN, None),
        P(),
    )
    return jax.shard_map(
        local,
        mesh=mesh,
        in_specs=placed,
        out_specs=(P(None, TIME, CHAN), P(None, None, TIME, CHAN), P(CHAN, TIME)),
        check_vma=False,
    )
```

```python
import jax
import jax.numpy as jnp
from jax import lax
from jax.sharding import PartitionSpec as P

DILATION_STEPS = 1024


TIME = ("tz", "tx", "tc")
CHAN = ("cy", "cx")


def shifted(x, axis, by):
    peers = lax.axis_size(axis[0]) * lax.axis_size(axis[1]) * lax.axis_size(axis[2])
    pairs = [(i, i + by) for i in range(peers) if 0 <= i + by < peers]
    return lax.ppermute(x, axis, pairs)


def contract_rows(left, right):
    return lax.dot_general(
        left, right, (((0,), (0,)), ((), ())), preferred_element_type=jnp.float32
    )


def contract_cols(left, right):
    return lax.dot_general(
        left, right, (((1,), (1,)), ((), ())), preferred_element_type=jnp.float32
    )


def ring_sum(chunks, axis):
    peers = lax.axis_size(axis)
    at = lax.axis_index(axis)
    half = chunks.shape[-1] // 2
    sums = []
    for step, cols in ((1, slice(0, half)), (-1, slice(half, None))):
        own = chunks[..., cols]
        pairs = [(i, (i + step) % peers) for i in range(peers)]
        acc = lax.dynamic_index_in_dim(own, (at - step) % peers, 0, keepdims=False)
        for s in range(peers - 1):
            got = lax.ppermute(acc, axis, pairs)
            acc = got + lax.dynamic_index_in_dim(
                own, (at - step * (s + 2)) % peers, 0, keepdims=False
            )
        sums.append(acc)
    return jnp.concatenate(sums, axis=-1)


def swap_sum(parts, axis):
    me = lax.axis_index(axis)
    keep = lax.dynamic_index_in_dim(parts, me, 0, keepdims=False)
    give = lax.dynamic_index_in_dim(parts, 1 - me, 0, keepdims=False)
    return keep + lax.ppermute(give, axis, [(0, 1), (1, 0)])


def chan_ring_reduce_scatter(x):
    peers = lax.axis_size("cy")
    at = lax.axis_index("cy")
    chunks = x.reshape(peers, x.shape[0] // peers, x.shape[1])
    half = x.shape[1] // 2
    sums = []
    for step, cols in ((1, slice(0, half)), (-1, slice(half, None))):
        own = chunks[:, :, cols]
        pairs = [(i, (i + step) % peers) for i in range(peers)]
        acc = lax.dynamic_index_in_dim(own, (at - step) % peers, 0, keepdims=False)
        for s in range(peers - 1):
            got = lax.ppermute(acc, "cy", pairs)
            acc = got + lax.dynamic_index_in_dim(
                own, (at - step * (s + 2)) % peers, 0, keepdims=False
            )
        sums.append(acc)
    full = jnp.concatenate(sums, axis=1)
    return swap_sum(full.reshape(2, full.shape[0] // 2, full.shape[1]), "cx")


def time_reduce_scatter(x):
    outer, mid, inner = (lax.axis_size(a) for a in TIME)
    blocks = x.reshape(outer, mid, inner, x.shape[0] // (outer * mid * inner), x.shape[1])
    blocks = swap_sum(jnp.moveaxis(blocks, 2, 0), TIME[2])
    blocks = ring_sum(blocks, TIME[0])
    return swap_sum(blocks, TIME[1])


def local(states, upstream, w_in, w_out, lengths):
    traj, window_extent, width = states.shape
    blocks = w_in.shape[3]
    rows_n = traj * window_extent
    receptive_extent = DILATION_STEPS // window_extent
    rows = states.reshape(rows_n, width)
    w_now = jnp.concatenate([w_in[0, 0], w_in[0, 1]], axis=1)
    w_dil = jnp.concatenate([w_in[1, 0], w_in[1, 1]], axis=1)
    dilated = jnp.dot(rows, w_dil, preferred_element_type=jnp.float32)
    present = jnp.dot(rows, w_now, preferred_element_type=jnp.float32)
    first = lax.axis_index(TIME) * window_extent
    positions = first + jnp.arange(window_extent, dtype=jnp.int32)
    valid = positions[None, :] < lengths[:, None]
    grad_rows = jnp.where(valid[:, :, None], upstream, jnp.zeros_like(upstream))
    grad_flat = grad_rows.reshape(rows_n, width)
    dmix = contract_cols(grad_flat, w_out)
    mixed_parts, grad_parts, later_parts = [], [], []
    for b in range(traj):
        rows_b = slice(b * window_extent, (b + 1) * window_extent)
        pre = present[rows_b] + shifted(dilated[rows_b], TIME, receptive_extent)
        tangent = jnp.tanh(pre[:, :blocks])
        sigma = jax.nn.sigmoid(pre[:, blocks:])
        mixed_parts.append((tangent * sigma).astype(jnp.bfloat16))
        dmix_b = dmix[rows_b]
        filter_gradient = (dmix_b * (1.0 - tangent * tangent) * sigma).astype(jnp.bfloat16)
        gate_gradient = (dmix_b * tangent * sigma * (1.0 - sigma)).astype(jnp.bfloat16)
        grad_b = jnp.concatenate([filter_gradient, gate_gradient], axis=1)
        grad_parts.append(grad_b)
        later_parts.append(shifted(grad_b, TIME, -receptive_extent))
    mixed = jnp.concatenate(mixed_parts, axis=0)
    branch_grads = jnp.concatenate(grad_parts, axis=0)
    later = jnp.concatenate(later_parts, axis=0)
    partial_value = contract_cols(w_now, branch_grads) + contract_cols(w_dil, later)
    cut = partial_value.shape[1] // 2
    summed = jnp.concatenate(
        [
            lax.psum_scatter(partial_value[:, :cut], CHAN, scatter_dimension=0, tiled=True),
            chan_ring_reduce_scatter(partial_value[:, cut:]),
        ],
        axis=1,
    )
    share = width // (lax.axis_size("cy") * lax.axis_size("cx"))
    own_rows = lax.dynamic_slice_in_dim(grad_rows, lax.axis_index(CHAN) * share, share, 2)
    summed = summed.reshape(share, traj, window_extent).transpose(1, 2, 0)
    grad_states = (own_rows.astype(jnp.float32) + summed).astype(jnp.bfloat16)
    zeros = jnp.zeros_like(branch_grads)
    right = jnp.concatenate(
        [
            jnp.concatenate([branch_grads, later, jnp.zeros_like(mixed)], axis=1),
            jnp.concatenate([zeros, zeros, mixed], axis=1),
        ],
        axis=0,
    )
    weight_terms = contract_rows(jnp.concatenate([rows, grad_flat], axis=0), right)
    reduced = time_reduce_scatter(weight_terms)
    scale = lax.rsqrt(jnp.sum(lengths.astype(jnp.float32)))
    part = reduced.shape[0]
    in_summed = reduced[:, : 4 * blocks].reshape(part, 2, 2, blocks).transpose(1, 2, 0, 3)
    out_summed = reduced[:, 4 * blocks :].T
    return (grad_states, in_summed * scale, out_summed * scale)


def solution(mesh):
    tm, chan = mesh.shape["tm"], mesh.shape["chan"]
    mesh = jax.sharding.Mesh(mesh.devices.reshape(tm // 4, 2, 2, chan // 2, 2), TIME + CHAN)
    placed = (
        P(None, TIME, None),
        P(None, TIME, None),
        P(None, None, None, CHAN),
        P(CHAN, None),
        P(),
    )
    return jax.shard_map(
        local,
        mesh=mesh,
        in_specs=placed,
        out_specs=(P(None, TIME, CHAN), P(None, None, TIME, CHAN), P(CHAN, TIME)),
        check_vma=False,
    )
```

```python
import jax
import jax.numpy as jnp
from jax import lax
from jax.sharding import PartitionSpec as P

DILATION_STEPS = 1024


TIME = ("tz", "tx", "tc")
CHAN = ("cy", "cx")


def shifted(x, axis, by):
    peers = lax.axis_size(axis[0]) * lax.axis_size(axis[1]) * lax.axis_size(axis[2])
    pairs = [(i, i + by) for i in range(peers) if 0 <= i + by < peers]
    return lax.ppermute(x, axis, pairs)


def contract_rows(left, right):
    return lax.dot_general(
        left, right, (((0,), (0,)), ((), ())), preferred_element_type=jnp.float32
    )


def contract_cols(left, right):
    return lax.dot_general(
        left, right, (((1,), (1,)), ((), ())), preferred_element_type=jnp.float32
    )


def ring_sum(chunks, axis):
    peers = lax.axis_size(axis)
    at = lax.axis_index(axis)
    half = chunks.shape[-1] // 2
    sums = []
    for step, cols in ((1, slice(0, half)), (-1, slice(half, None))):
        own = chunks[..., cols]
        pairs = [(i, (i + step) % peers) for i in range(peers)]
        acc = lax.dynamic_index_in_dim(own, (at - step) % peers, 0, keepdims=False)
        for s in range(peers - 1):
            got = lax.ppermute(acc, axis, pairs)
            acc = got + lax.dynamic_index_in_dim(
                own, (at - step * (s + 2)) % peers, 0, keepdims=False
            )
        sums.append(acc)
    return jnp.concatenate(sums, axis=-1)


def swap_sum(parts, axis):
    me = lax.axis_index(axis)
    keep = lax.dynamic_index_in_dim(parts, me, 0, keepdims=False)
    give = lax.dynamic_index_in_dim(parts, 1 - me, 0, keepdims=False)
    return keep + lax.ppermute(give, axis, [(0, 1), (1, 0)])


def chan_ring_reduce_scatter(x):
    peers = lax.axis_size("cy")
    at = lax.axis_index("cy")
    chunks = x.reshape(peers, x.shape[0] // peers, x.shape[1])
    half = x.shape[1] // 2
    sums = []
    for step, cols in ((1, slice(0, half)), (-1, slice(half, None))):
        own = chunks[:, :, cols]
        pairs = [(i, (i + step) % peers) for i in range(peers)]
        acc = lax.dynamic_index_in_dim(own, (at - step) % peers, 0, keepdims=False)
        for s in range(peers - 1):
            got = lax.ppermute(acc, "cy", pairs)
            acc = got + lax.dynamic_index_in_dim(
                own, (at - step * (s + 2)) % peers, 0, keepdims=False
            )
        sums.append(acc)
    full = jnp.concatenate(sums, axis=1)
    return swap_sum(full.reshape(2, full.shape[0] // 2, full.shape[1]), "cx")


def time_reduce_scatter(x):
    outer, mid, inner = (lax.axis_size(a) for a in TIME)
    blocks = x.reshape(outer, mid, inner, x.shape[0] // (outer * mid * inner), x.shape[1])
    blocks = swap_sum(jnp.moveaxis(blocks, 2, 0), TIME[2])
    blocks = ring_sum(blocks, TIME[0])
    return swap_sum(blocks, TIME[1])


def local(states, upstream, w_in, w_out, lengths):
    traj, window_extent, width = states.shape
    blocks = w_in.shape[3]
    rows_n = traj * window_extent
    receptive_extent = DILATION_STEPS // window_extent
    rows = states.reshape(rows_n, width)
    w_now = jnp.concatenate([w_in[0, 0], w_in[0, 1]], axis=1)
    w_dil = jnp.concatenate([w_in[1, 0], w_in[1, 1]], axis=1)
    dilated = jnp.dot(rows, w_dil, preferred_element_type=jnp.float32)
    present = jnp.dot(rows, w_now, preferred_element_type=jnp.float32)
    first = lax.axis_index(TIME) * window_extent
    positions = first + jnp.arange(window_extent, dtype=jnp.int32)
    valid = positions[None, :] < lengths[:, None]
    grad_rows = jnp.where(valid[:, :, None], upstream, jnp.zeros_like(upstream))
    grad_flat = grad_rows.reshape(rows_n, width)
    dmix = contract_cols(grad_flat, w_out)
    mixed_parts, grad_parts, later_parts = [], [], []
    piece = window_extent // 2
    for b in range(rows_n // piece):
        rows_b = slice(b * piece, (b + 1) * piece)
        pre = present[rows_b] + shifted(dilated[rows_b], TIME, receptive_extent)
        tangent = jnp.tanh(pre[:, :blocks])
        sigma = jax.nn.sigmoid(pre[:, blocks:])
        mixed_parts.append((tangent * sigma).astype(jnp.bfloat16))
        dmix_b = dmix[rows_b]
        filter_gradient = (dmix_b * (1.0 - tangent * tangent) * sigma).astype(jnp.bfloat16)
        gate_gradient = (dmix_b * tangent * sigma * (1.0 - sigma)).astype(jnp.bfloat16)
        grad_b = jnp.concatenate([filter_gradient, gate_gradient], axis=1)
        grad_parts.append(grad_b)
        later_parts.append(shifted(grad_b, TIME, -receptive_extent))
    mixed = jnp.concatenate(mixed_parts, axis=0)
    branch_grads = jnp.concatenate(grad_parts, axis=0)
    later = jnp.concatenate(later_parts, axis=0)
    partial_value = contract_cols(w_now, branch_grads) + contract_cols(w_dil, later)
    cut = partial_value.shape[1] // 2
    summed = jnp.concatenate(
        [
            lax.psum_scatter(partial_value[:, :cut], CHAN, scatter_dimension=0, tiled=True),
            chan_ring_reduce_scatter(partial_value[:, cut:]),
        ],
        axis=1,
    )
    share = width // (lax.axis_size("cy") * lax.axis_size("cx"))
    own_rows = lax.dynamic_slice_in_dim(grad_rows, lax.axis_index(CHAN) * share, share, 2)
    summed = summed.reshape(share, traj, window_extent).transpose(1, 2, 0)
    grad_states = (own_rows.astype(jnp.float32) + summed).astype(jnp.bfloat16)
    zeros = jnp.zeros_like(branch_grads)
    right = jnp.concatenate(
        [
            jnp.concatenate([branch_grads, later, jnp.zeros_like(mixed)], axis=1),
            jnp.concatenate([zeros, zeros, mixed], axis=1),
        ],
        axis=0,
    )
    weight_terms = contract_rows(jnp.concatenate([rows, grad_flat], axis=0), right)
    reduced = time_reduce_scatter(weight_terms)
    scale = lax.rsqrt(jnp.sum(lengths.astype(jnp.float32)))
    part = reduced.shape[0]
    in_summed = reduced[:, : 4 * blocks].reshape(part, 2, 2, blocks).transpose(1, 2, 0, 3)
    out_summed = reduced[:, 4 * blocks :].T
    return (grad_states, in_summed * scale, out_summed * scale)


def solution(mesh):
    tm, chan = mesh.shape["tm"], mesh.shape["chan"]
    mesh = jax.sharding.Mesh(mesh.devices.reshape(tm // 4, 2, 2, chan // 2, 2), TIME + CHAN)
    placed = (
        P(None, TIME, None),
        P(None, TIME, None),
        P(None, None, None, CHAN),
        P(CHAN, None),
        P(),
    )
    return jax.shard_map(
        local,
        mesh=mesh,
        in_specs=placed,
        out_specs=(P(None, TIME, CHAN), P(None, None, TIME, CHAN), P(CHAN, TIME)),
        check_vma=False,
    )
```

```python
import jax
import jax.numpy as jnp
from jax import lax
from jax.sharding import PartitionSpec as P

DILATION_STEPS = 1024


TIME = ("tz", "tx", "tc")
CHAN = ("cy", "cx")


def shifted(x, axis, by):
    peers = lax.axis_size(axis[0]) * lax.axis_size(axis[1]) * lax.axis_size(axis[2])
    pairs = [(i, i + by) for i in range(peers) if 0 <= i + by < peers]
    return lax.ppermute(x, axis, pairs)


def contract_rows(left, right):
    return lax.dot_general(
        left, right, (((0,), (0,)), ((), ())), preferred_element_type=jnp.float32
    )


def contract_cols(left, right):
    return lax.dot_general(
        left, right, (((1,), (1,)), ((), ())), preferred_element_type=jnp.float32
    )


def ring_sum(chunks, axis):
    peers = lax.axis_size(axis)
    at = lax.axis_index(axis)
    sums = []
    for step, half in ((1, 0), (-1, 1)):
        own = chunks[:, half]
        pairs = [(i, (i + step) % peers) for i in range(peers)]
        acc = lax.dynamic_index_in_dim(own, (at - step) % peers, 0, keepdims=False)
        for s in range(peers - 1):
            got = lax.ppermute(acc, axis, pairs)
            acc = got + lax.dynamic_index_in_dim(
                own, (at - step * (s + 2)) % peers, 0, keepdims=False
            )
        sums.append(acc)
    return jnp.stack(sums)


def swap_sum(parts, axis):
    me = lax.axis_index(axis)
    keep = lax.dynamic_index_in_dim(parts, me, 0, keepdims=False)
    give = lax.dynamic_index_in_dim(parts, 1 - me, 0, keepdims=False)
    return keep + lax.ppermute(give, axis, [(0, 1), (1, 0)])


def chan_ring_reduce_scatter(x):
    peers = lax.axis_size("cy")
    at = lax.axis_index("cy")
    chunks = x.reshape(peers, x.shape[0] // peers, x.shape[1])
    half = x.shape[1] // 2
    sums = []
    for step, cols in ((1, slice(0, half)), (-1, slice(half, None))):
        own = chunks[:, :, cols]
        pairs = [(i, (i + step) % peers) for i in range(peers)]
        acc = lax.dynamic_index_in_dim(own, (at - step) % peers, 0, keepdims=False)
        for s in range(peers - 1):
            got = lax.ppermute(acc, "cy", pairs)
            acc = got + lax.dynamic_index_in_dim(
                own, (at - step * (s + 2)) % peers, 0, keepdims=False
            )
        sums.append(acc)
    full = jnp.concatenate(sums, axis=1)
    return swap_sum(full.reshape(2, full.shape[0] // 2, full.shape[1]), "cx")


def time_reduce_scatter(x):
    outer, mid, inner = (lax.axis_size(a) for a in TIME)
    blocks = x.reshape(outer, mid, inner, x.shape[0] // (outer * mid * inner), x.shape[1])
    blocks = swap_sum(jnp.moveaxis(blocks, 2, 0), TIME[2])
    blocks = ring_sum(blocks, TIME[0])
    return swap_sum(blocks, TIME[1])


def local(states, upstream, w_in, w_out, lengths):
    traj, window_extent, width = states.shape
    blocks = w_in.shape[3]
    rows_n = traj * window_extent
    receptive_extent = DILATION_STEPS // window_extent
    rows = states.reshape(rows_n, width)
    w_now = jnp.concatenate([w_in[0, 0], w_in[0, 1]], axis=1)
    w_dil = jnp.concatenate([w_in[1, 0], w_in[1, 1]], axis=1)
    dilated = jnp.dot(rows, w_dil, preferred_element_type=jnp.float32)
    present = jnp.dot(rows, w_now, preferred_element_type=jnp.float32)
    first = lax.axis_index(TIME) * window_extent
    positions = first + jnp.arange(window_extent, dtype=jnp.int32)
    valid = positions[None, :] < lengths[:, None]
    grad_rows = jnp.where(valid[:, :, None], upstream, jnp.zeros_like(upstream))
    grad_flat = grad_rows.reshape(rows_n, width)
    dmix = contract_cols(grad_flat, w_out)
    mixed_parts, grad_parts, later_parts = [], [], []
    for b in range(traj):
        rows_b = slice(b * window_extent, (b + 1) * window_extent)
        pre = present[rows_b] + shifted(dilated[rows_b], TIME, receptive_extent)
        tangent = jnp.tanh(pre[:, :blocks])
        sigma = jax.nn.sigmoid(pre[:, blocks:])
        mixed_parts.append((tangent * sigma).astype(jnp.bfloat16))
        dmix_b = dmix[rows_b]
        filter_gradient = (dmix_b * (1.0 - tangent * tangent) * sigma).astype(jnp.bfloat16)
        gate_gradient = (dmix_b * tangent * sigma * (1.0 - sigma)).astype(jnp.bfloat16)
        grad_b = jnp.concatenate([filter_gradient, gate_gradient], axis=1)
        grad_parts.append(grad_b)
        later_parts.append(shifted(grad_b, TIME, -receptive_extent))
    mixed = jnp.concatenate(mixed_parts, axis=0)
    branch_grads = jnp.concatenate(grad_parts, axis=0)
    later = jnp.concatenate(later_parts, axis=0)
    partial_value = contract_cols(w_now, branch_grads) + contract_cols(w_dil, later)
    cut = partial_value.shape[1] // 2
    summed = jnp.concatenate(
        [
            lax.psum_scatter(partial_value[:, :cut], CHAN, scatter_dimension=0, tiled=True),
            chan_ring_reduce_scatter(partial_value[:, cut:]),
        ],
        axis=1,
    )
    share = width // (lax.axis_size("cy") * lax.axis_size("cx"))
    own_rows = lax.dynamic_slice_in_dim(grad_rows, lax.axis_index(CHAN) * share, share, 2)
    summed = summed.reshape(share, traj, window_extent).transpose(1, 2, 0)
    grad_states = (own_rows.astype(jnp.float32) + summed).astype(jnp.bfloat16)
    zeros = jnp.zeros_like(branch_grads)
    right = jnp.concatenate(
        [
            jnp.concatenate([branch_grads, later, jnp.zeros_like(mixed)], axis=1),
            jnp.concatenate([zeros, zeros, mixed], axis=1),
        ],
        axis=0,
    )
    weight_terms = contract_rows(jnp.concatenate([rows, grad_flat], axis=0), right)
    reduced = time_reduce_scatter(weight_terms)
    scale = lax.rsqrt(jnp.sum(lengths.astype(jnp.float32)))
    part = reduced.shape[0]
    in_summed = reduced[:, : 4 * blocks].reshape(part, 2, 2, blocks).transpose(1, 2, 0, 3)
    out_summed = reduced[:, 4 * blocks :].T
    return (grad_states, in_summed * scale, out_summed * scale)


def solution(mesh):
    tm, chan = mesh.shape["tm"], mesh.shape["chan"]
    mesh = jax.sharding.Mesh(mesh.devices.reshape(tm // 4, 2, 2, chan // 2, 2), TIME + CHAN)
    placed = (
        P(None, TIME, None),
        P(None, TIME, None),
        P(None, None, None, CHAN),
        P(CHAN, None),
        P(),
    )
    return jax.shard_map(
        local,
        mesh=mesh,
        in_specs=placed,
        out_specs=(P(None, TIME, CHAN), P(None, None, TIME, CHAN), P(CHAN, TIME)),
        check_vma=False,
    )
```

```python
import jax
import jax.numpy as jnp
from jax import lax
from jax.sharding import PartitionSpec as P

DILATION_STEPS = 1024


TIME = ("tz", "tx", "tc")
CHAN = ("cy", "cx")


def shifted(x, axis, by):
    peers = lax.axis_size(axis[0]) * lax.axis_size(axis[1]) * lax.axis_size(axis[2])
    pairs = [(i, i + by) for i in range(peers) if 0 <= i + by < peers]
    return lax.ppermute(x, axis, pairs)


def contract_rows(left, right):
    return lax.dot_general(
        left, right, (((0,), (0,)), ((), ())), preferred_element_type=jnp.float32
    )


def contract_cols(left, right):
    return lax.dot_general(
        left, right, (((1,), (1,)), ((), ())), preferred_element_type=jnp.float32
    )


def ring_sum(chunks, axis):
    peers = lax.axis_size(axis)
    at = lax.axis_index(axis)
    half = chunks.shape[-1] // 2
    sums = []
    for step, cols in ((1, slice(0, half)), (-1, slice(half, None))):
        own = chunks[..., cols]
        pairs = [(i, (i + step) % peers) for i in range(peers)]
        acc = lax.dynamic_index_in_dim(own, (at - step) % peers, 0, keepdims=False)
        for s in range(peers - 1):
            got = lax.ppermute(acc, axis, pairs)
            acc = got + lax.dynamic_index_in_dim(
                own, (at - step * (s + 2)) % peers, 0, keepdims=False
            )
        sums.append(acc)
    return jnp.concatenate(sums, axis=-1)


def swap_sum(parts, axis):
    me = lax.axis_index(axis)
    keep = lax.dynamic_index_in_dim(parts, me, 0, keepdims=False)
    give = lax.dynamic_index_in_dim(parts, 1 - me, 0, keepdims=False)
    return keep + lax.ppermute(give, axis, [(0, 1), (1, 0)])


def chan_ring_reduce_scatter(x):
    peers = lax.axis_size("cy")
    at = lax.axis_index("cy")
    chunks = x.reshape(peers, x.shape[0] // peers, x.shape[1])
    half = x.shape[1] // 2
    sums = []
    for step, cols in ((1, slice(0, half)), (-1, slice(half, None))):
        own = chunks[:, :, cols]
        pairs = [(i, (i + step) % peers) for i in range(peers)]
        acc = lax.dynamic_index_in_dim(own, (at - step) % peers, 0, keepdims=False)
        for s in range(peers - 1):
            got = lax.ppermute(acc, "cy", pairs)
            acc = got + lax.dynamic_index_in_dim(
                own, (at - step * (s + 2)) % peers, 0, keepdims=False
            )
        sums.append(acc)
    full = jnp.concatenate(sums, axis=1)
    return swap_sum(full.reshape(2, full.shape[0] // 2, full.shape[1]), "cx")


def time_reduce_scatter(x):
    outer, mid, inner = (lax.axis_size(a) for a in TIME)
    blocks = x.reshape(outer, mid, inner, x.shape[0] // (outer * mid * inner), x.shape[1])
    blocks = swap_sum(jnp.moveaxis(blocks, 2, 0), TIME[2])
    blocks = ring_sum(blocks, TIME[0])
    return swap_sum(blocks, TIME[1])


def local(states, upstream, w_in, w_out, lengths):
    traj, window_extent, width = states.shape
    blocks = w_in.shape[3]
    rows_n = traj * window_extent
    receptive_extent = DILATION_STEPS // window_extent
    rows = states.reshape(rows_n, width)
    w_now = jnp.concatenate([w_in[0, 0], w_in[0, 1]], axis=1)
    w_dil = jnp.concatenate([w_in[1, 0], w_in[1, 1]], axis=1)
    dilated = jnp.dot(rows, w_dil, preferred_element_type=jnp.float32)
    present = jnp.dot(rows, w_now, preferred_element_type=jnp.float32)
    first = lax.axis_index(TIME) * window_extent
    positions = first + jnp.arange(window_extent, dtype=jnp.int32)
    valid = positions[None, :] < lengths[:, None]
    grad_rows = jnp.where(valid[:, :, None], upstream, jnp.zeros_like(upstream))
    grad_flat = grad_rows.reshape(rows_n, width)
    dmix = contract_cols(grad_flat, w_out)
    mixed_parts, grad_parts, later_parts = [], [], []
    for b in range(traj):
        rows_b = slice(b * window_extent, (b + 1) * window_extent)
        pre = present[rows_b] + shifted(dilated[rows_b], TIME, receptive_extent)
        tangent = jnp.tanh(pre[:, :blocks])
        sigma = jax.nn.sigmoid(pre[:, blocks:])
        mixed_parts.append((tangent * sigma).astype(jnp.bfloat16))
        dmix_b = dmix[rows_b]
        filter_gradient = (dmix_b * (1.0 - tangent * tangent) * sigma).astype(jnp.bfloat16)
        gate_gradient = (dmix_b * tangent * sigma * (1.0 - sigma)).astype(jnp.bfloat16)
        grad_b = jnp.concatenate([filter_gradient, gate_gradient], axis=1)
        grad_parts.append(grad_b)
        later_parts.append(shifted(grad_b, TIME, -receptive_extent))
    mixed = jnp.concatenate(mixed_parts, axis=0)
    branch_grads = jnp.concatenate(grad_parts, axis=0)
    later = jnp.concatenate(later_parts, axis=0)
    partial_value = contract_cols(w_now, branch_grads) + contract_cols(w_dil, later)
    cut = partial_value.shape[1] * 3 // 4
    summed = jnp.concatenate(
        [
            lax.psum_scatter(partial_value[:, :cut], CHAN, scatter_dimension=0, tiled=True),
            chan_ring_reduce_scatter(partial_value[:, cut:]),
        ],
        axis=1,
    )
    share = width // (lax.axis_size("cy") * lax.axis_size("cx"))
    own_rows = lax.dynamic_slice_in_dim(grad_rows, lax.axis_index(CHAN) * share, share, 2)
    summed = summed.reshape(share, traj, window_extent).transpose(1, 2, 0)
    grad_states = (own_rows.astype(jnp.float32) + summed).astype(jnp.bfloat16)
    zeros = jnp.zeros_like(branch_grads)
    right = jnp.concatenate(
        [
            jnp.concatenate([branch_grads, later, jnp.zeros_like(mixed)], axis=1),
            jnp.concatenate([zeros, zeros, mixed], axis=1),
        ],
        axis=0,
    )
    weight_terms = contract_rows(jnp.concatenate([rows, grad_flat], axis=0), right)
    reduced = time_reduce_scatter(weight_terms)
    scale = lax.rsqrt(jnp.sum(lengths.astype(jnp.float32)))
    part = reduced.shape[0]
    in_summed = reduced[:, : 4 * blocks].reshape(part, 2, 2, blocks).transpose(1, 2, 0, 3)
    out_summed = reduced[:, 4 * blocks :].T
    return (grad_states, in_summed * scale, out_summed * scale)


def solution(mesh):
    tm, chan = mesh.shape["tm"], mesh.shape["chan"]
    mesh = jax.sharding.Mesh(mesh.devices.reshape(tm // 4, 2, 2, chan // 2, 2), TIME + CHAN)
    placed = (
        P(None, TIME, None),
        P(None, TIME, None),
        P(None, None, None, CHAN),
        P(CHAN, None),
        P(),
    )
    return jax.shard_map(
        local,
        mesh=mesh,
        in_specs=placed,
        out_specs=(P(None, TIME, CHAN), P(None, None, TIME, CHAN), P(CHAN, TIME)),
        check_vma=False,
    )
```

```python
import jax
import jax.numpy as jnp
from jax import lax
from jax.sharding import PartitionSpec as P

DILATION_STEPS = 1024


TIME = ("tz", "tx", "tc")
CHAN = ("cy", "cx")


def shifted(x, axis, by):
    peers = lax.axis_size(axis[0]) * lax.axis_size(axis[1]) * lax.axis_size(axis[2])
    pairs = [(i, i + by) for i in range(peers) if 0 <= i + by < peers]
    return lax.ppermute(x, axis, pairs)


def contract_rows(left, right):
    return lax.dot_general(
        left, right, (((0,), (0,)), ((), ())), preferred_element_type=jnp.float32
    )


def contract_cols(left, right):
    return lax.dot_general(
        left, right, (((1,), (1,)), ((), ())), preferred_element_type=jnp.float32
    )


def ring_sum(chunks, axis):
    peers = lax.axis_size(axis)
    at = lax.axis_index(axis)
    half = chunks.shape[-1] // 2
    sums = []
    for step, cols in ((1, slice(0, half)), (-1, slice(half, None))):
        own = chunks[..., cols]
        pairs = [(i, (i + step) % peers) for i in range(peers)]
        acc = lax.dynamic_index_in_dim(own, (at - step) % peers, 0, keepdims=False)
        for s in range(peers - 1):
            got = lax.ppermute(acc, axis, pairs)
            acc = got + lax.dynamic_index_in_dim(
                own, (at - step * (s + 2)) % peers, 0, keepdims=False
            )
        sums.append(acc)
    return jnp.concatenate(sums, axis=-1)


def swap_sum(parts, axis):
    me = lax.axis_index(axis)
    keep = lax.dynamic_index_in_dim(parts, me, 0, keepdims=False)
    give = lax.dynamic_index_in_dim(parts, 1 - me, 0, keepdims=False)
    return keep + lax.ppermute(give, axis, [(0, 1), (1, 0)])


def chan_ring_reduce_scatter(x):
    peers = lax.axis_size("cy")
    at = lax.axis_index("cy")
    chunks = x.reshape(peers, x.shape[0] // peers, x.shape[1])
    half = x.shape[1] // 2
    sums = []
    for step, cols in ((1, slice(0, half)), (-1, slice(half, None))):
        own = chunks[:, :, cols]
        pairs = [(i, (i + step) % peers) for i in range(peers)]
        acc = lax.dynamic_index_in_dim(own, (at - step) % peers, 0, keepdims=False)
        for s in range(peers - 1):
            got = lax.ppermute(acc, "cy", pairs)
            acc = got + lax.dynamic_index_in_dim(
                own, (at - step * (s + 2)) % peers, 0, keepdims=False
            )
        sums.append(acc)
    full = jnp.concatenate(sums, axis=1)
    return swap_sum(full.reshape(2, full.shape[0] // 2, full.shape[1]), "cx")


def time_reduce_scatter(x):
    outer, mid, inner = (lax.axis_size(a) for a in TIME)
    blocks = x.reshape(outer, mid, inner, x.shape[0] // (outer * mid * inner), x.shape[1])
    blocks = swap_sum(jnp.moveaxis(blocks, 2, 0), TIME[2])
    blocks = ring_sum(blocks, TIME[0])
    return swap_sum(blocks, TIME[1])


def local(states, upstream, w_in, w_out, lengths):
    traj, window_extent, width = states.shape
    blocks = w_in.shape[3]
    rows_n = traj * window_extent
    receptive_extent = DILATION_STEPS // window_extent
    rows = states.reshape(rows_n, width)
    w_now = jnp.concatenate([w_in[0, 0], w_in[0, 1]], axis=1)
    w_dil = jnp.concatenate([w_in[1, 0], w_in[1, 1]], axis=1)
    dilated = jnp.dot(rows, w_dil, preferred_element_type=jnp.float32)
    present = jnp.dot(rows, w_now, preferred_element_type=jnp.float32)
    first = lax.axis_index(TIME) * window_extent
    positions = first + jnp.arange(window_extent, dtype=jnp.int32)
    valid = positions[None, :] < lengths[:, None]
    grad_rows = jnp.where(valid[:, :, None], upstream, jnp.zeros_like(upstream))
    grad_flat = grad_rows.reshape(rows_n, width)
    dmix = contract_cols(grad_flat, w_out)
    mixed_parts, grad_parts, later_parts = [], [], []
    for b in range(traj):
        rows_b = slice(b * window_extent, (b + 1) * window_extent)
        pre = present[rows_b] + shifted(dilated[rows_b], TIME, receptive_extent)
        tangent = jnp.tanh(pre[:, :blocks])
        sigma = jax.nn.sigmoid(pre[:, blocks:])
        mixed_parts.append((tangent * sigma).astype(jnp.bfloat16))
        dmix_b = dmix[rows_b]
        filter_gradient = (dmix_b * (1.0 - tangent * tangent) * sigma).astype(jnp.bfloat16)
        gate_gradient = (dmix_b * tangent * sigma * (1.0 - sigma)).astype(jnp.bfloat16)
        grad_b = jnp.concatenate([filter_gradient, gate_gradient], axis=1)
        grad_parts.append(grad_b)
        later_parts.append(shifted(grad_b, TIME, -receptive_extent))
    mixed = jnp.concatenate(mixed_parts, axis=0)
    branch_grads = jnp.concatenate(grad_parts, axis=0)
    later = jnp.concatenate(later_parts, axis=0)
    partial_value = contract_cols(w_now, branch_grads) + contract_cols(w_dil, later)
    cut = partial_value.shape[1] // 4
    summed = jnp.concatenate(
        [
            lax.psum_scatter(partial_value[:, :cut], CHAN, scatter_dimension=0, tiled=True),
            chan_ring_reduce_scatter(partial_value[:, cut:]),
        ],
        axis=1,
    )
    share = width // (lax.axis_size("cy") * lax.axis_size("cx"))
    own_rows = lax.dynamic_slice_in_dim(grad_rows, lax.axis_index(CHAN) * share, share, 2)
    summed = summed.reshape(share, traj, window_extent).transpose(1, 2, 0)
    grad_states = (own_rows.astype(jnp.float32) + summed).astype(jnp.bfloat16)
    zeros = jnp.zeros_like(branch_grads)
    right = jnp.concatenate(
        [
            jnp.concatenate([branch_grads, later, jnp.zeros_like(mixed)], axis=1),
            jnp.concatenate([zeros, zeros, mixed], axis=1),
        ],
        axis=0,
    )
    weight_terms = contract_rows(jnp.concatenate([rows, grad_flat], axis=0), right)
    reduced = time_reduce_scatter(weight_terms)
    scale = lax.rsqrt(jnp.sum(lengths.astype(jnp.float32)))
    part = reduced.shape[0]
    in_summed = reduced[:, : 4 * blocks].reshape(part, 2, 2, blocks).transpose(1, 2, 0, 3)
    out_summed = reduced[:, 4 * blocks :].T
    return (grad_states, in_summed * scale, out_summed * scale)


def solution(mesh):
    tm, chan = mesh.shape["tm"], mesh.shape["chan"]
    mesh = jax.sharding.Mesh(mesh.devices.reshape(tm // 4, 2, 2, chan // 2, 2), TIME + CHAN)
    placed = (
        P(None, TIME, None),
        P(None, TIME, None),
        P(None, None, None, CHAN),
        P(CHAN, None),
        P(),
    )
    return jax.shard_map(
        local,
        mesh=mesh,
        in_specs=placed,
        out_specs=(P(None, TIME, CHAN), P(None, None, TIME, CHAN), P(CHAN, TIME)),
        check_vma=False,
    )
```
